256 devices in a mesh: gx: 64 (over z, x, core), gy: 4 (over y).
Axes of the slice: x: 4, y: 4, z: 8, core: 2. Of those that a mesh axis runs over, the one named last changes fastest.
Arguments:
- volume: bfloat16 [128, 16, 128, 256], P('gx', 'gy'), may hold values from -40 to 40
- void_mask: int32 [128, 16, 128], P('gx', 'gy'), may hold values from 0 to 1, as said below
- kernel: bfloat16 [27, 256], replicated, may hold values from -1.25 to 1.25
- mix_weight: bfloat16 [4, 64, 64], replicated, may hold values from -0.75 to 0.75
- norm_gain: float32 [256], replicated, may hold values from 0.25 to 1.75
- upstream: bfloat16 [128, 16, 128, 256], P('gx', 'gy'), may hold values from -6 to 6
Outputs:
- output: bfloat16 [128, 16, 128, 256], P('gx', 'gy')
- volume_grad: bfloat16 [128, 16, 128, 256], P('gx', 'gy')
- kernel_grad: float32 [27, 256], replicated
- mix_grad: float32 [4, 64, 64], replicated
The draws below stay inside these ranges and needn't reach their ends.
Inputs may be any that keep to these rules, and one draw needn't show every extreme that they name: `void_mask`: 1 marks a void voxel; voxels whose third index is a multiple of 8 are never void.
All inputs are finite; a program needn't handle non-finite values.
Results may differ from the reference program's by a relative error of at most 0.0017.
The reference program's roundings to bfloat16 on the way (of `field`, `active` and `dfield`) count: a program that leaves them out, or rounds other values in their place, can miss the bound.
Values may be sent and summed in bfloat16 or wider, within the bound.
No kernel may reach another device: no remote copies, remote signals or barrier semaphores. Data moves between devices by JAX's collectives and lax.ppermute only.
A program may use at most 128 MiB of HBM per device.

```python
import math
import jax
import jax.numpy as jnp
from jax import lax

Z = 128
C = 256
GS = 64
SWEEPS = 5
G = 4
NX = 128
NY = 16
NVOX = 262144


def volume_values(key):
    keys = jax.random.split(key, 7)
    chan = jnp.exp(jax.random.uniform(keys[0], (C,), minval=math.log(0.35), maxval=math.log(3.5)))
    voxel = jnp.exp(jax.random.uniform(keys[1], (NX, NY, Z, 1), minval=math.log(0.35), maxval=math.log(3.5)))
    loading = jax.random.normal(keys[2], (C,))
    signs = jnp.where(jax.random.bernoulli(keys[5], 0.5, (C,)), 1.0, -1.0)
    offset = signs * jnp.exp(jax.random.uniform(keys[6], (C,), minval=math.log(0.5), maxval=math.log(2.0)))
    ramp_y = 1.0 + 2.0 * jnp.arange(NY, dtype=jnp.float32).reshape(1, NY, 1, 1) / max(NY - 1, 1)
    noise = jax.random.normal(keys[3], (NX, NY, Z, C))
    common = jax.random.normal(keys[4], (NX, NY, Z, 1))
    values = voxel * ramp_y * chan * (noise + 0.8 * common * loading + offset)
    return (jnp.clip(values, -40.0, 40.0), chan)


def draw_volume(key, part):
    values, chan = volume_values(jax.random.fold_in(key, 1))
    return values.astype(jnp.bfloat16)


def draw_upstream(key, part):
    values, chan = volume_values(jax.random.fold_in(key, 1))
    keys = jax.random.split(jax.random.fold_in(key, 2), 3)
    signs = jnp.where(jax.random.bernoulli(keys[0], 0.5, (C,)), 1.0, -1.0)
    factor = signs * jnp.exp(jax.random.uniform(keys[1], (C,), minval=math.log(0.3), maxval=math.log(0.9)))
    noise = jax.random.normal(keys[2], (NX, NY, Z, C))
    return jnp.clip(factor * values / chan + noise, -6.0, 6.0).astype(jnp.bfloat16)


def draw_void_mask(key, part):
    draws = jax.random.randint(key, (NX, NY, Z), 0, 1000)
    first = lax.broadcasted_iota(jnp.int32, (NX, NY, Z), 0)
    depth = lax.broadcasted_iota(jnp.int32, (NX, NY, Z), 2)
    keep_permille = 250 + 500 * first // max(NX - 1, 1)
    return jnp.where((draws >= keep_permille) & (depth % 8 != 0), 1, 0).astype(jnp.int32)


def normal_values(key, dims, width, limit, kind=jnp.bfloat16):
    return jnp.clip(width * jax.random.normal(key, dims, jnp.float32), -limit, limit).astype(kind)


def setup_inputs(seed: int = 0) -> dict:
    streams_of = jax.random.split(jax.random.key(seed), 7)
    return {
        "volume": draw_volume(jax.random.fold_in(streams_of[6], 71), 0),
        "void_mask": draw_void_mask(jax.random.fold_in(streams_of[6], 71), 0),
        "kernel": normal_values(streams_of[2], (27, C), 27 ** -0.5, 1.25),
        "mix_weight": normal_values(streams_of[3], (G, GS, GS), GS ** -0.5, 0.75),
        "norm_gain": jnp.clip(1.0 + 0.15 * jax.random.normal(streams_of[4], (C,), jnp.float32), 0.25, 1.75),
        "upstream": draw_upstream(jax.random.fold_in(streams_of[6], 71), 0),
    }


HI = lax.Precision.HIGHEST
EPS = 1e-05

def whiten(sigma):
    eye = jnp.eye(sigma.shape[0], dtype=sigma.dtype)
    trace = jnp.trace(sigma)
    scaled = sigma / trace
    proj = eye
    for sweep in range(SWEEPS):
        cube = jnp.dot(proj, jnp.dot(proj, jnp.dot(proj, scaled, precision=HI), precision=HI), precision=HI)
        proj = 1.5 * proj - 0.5 * cube
    return proj / jnp.sqrt(trace)

def shifted(field, tap, sign):
    ox, oy, oz = (tap // 9, tap // 3 % 3, tap % 3)
    return jnp.roll(field, (sign * (1 - ox), sign * (1 - oy), sign * (1 - oz)), axis=(0, 1, 2))

def reference(volume, void_mask, kernel, mix_weight, norm_gain, upstream):
    keep = (1 - void_mask).astype(jnp.float32)
    count = jnp.sum(keep)
    scale = float(NVOX)
    keep_rows = keep.reshape(-1, 1)
    vol_groups = jnp.moveaxis(volume.reshape(NX, NY, Z, G, GS), 3, 0)
    grad_groups = jnp.moveaxis(upstream.reshape(NX, NY, Z, G, GS), 3, 0)
    ker_groups = jnp.moveaxis(kernel.reshape(27, G, GS), 1, 0)
    gain_groups = norm_gain.reshape(G, GS)

    def one_group(items):
        vol, ker, mix, gain, grad = items
        vol_f = vol.astype(jnp.float32)
        ker_f = ker.astype(jnp.float32)
        total = jnp.zeros((NX, NY, Z, GS), jnp.float32)
        for tap in range(27):
            total = total + shifted(vol_f, tap, 1) * ker_f[tap]
        field = lax.optimization_barrier(total.astype(jnp.bfloat16)).astype(jnp.float32)
        mean = lax.optimization_barrier(jnp.sum(keep[..., None] * field, axis=(0, 1, 2))) / count
        rows = (field - mean).reshape(-1, GS)
        sigma = jnp.dot((keep_rows * rows).T, rows, precision=HI) / count + EPS * jnp.eye(GS, dtype=jnp.float32)
        white = whiten(sigma)
        pre = jnp.dot(rows, white.T, precision=HI) * gain
        active = jax.nn.silu(pre).astype(jnp.bfloat16)
        grad_rows = grad.reshape(-1, GS)
        out = (vol.reshape(-1, GS).astype(jnp.float32) + jnp.dot(active, mix, preferred_element_type=jnp.float32)).astype(jnp.bfloat16)
        dact = jnp.dot(grad_rows, mix.T, preferred_element_type=jnp.float32)
        sig = jax.nn.sigmoid(pre)
        dnormed = dact * sig * (1.0 + pre * (1.0 - sig)) * gain
        dwhite = jnp.dot(dnormed.T, rows, precision=HI)
        dcent = jnp.dot(dnormed, white, precision=HI)
        sens = jax.vjp(whiten, sigma)[1](dwhite)[0]
        sym = sens + sens.T
        dsum = lax.optimization_barrier(jnp.sum(dcent, axis=0))
        dfield = dcent + keep_rows / count * (jnp.dot(rows, sym, precision=HI) - dsum)
        dfield = lax.optimization_barrier(dfield.astype(jnp.bfloat16)).reshape(NX, NY, Z, GS).astype(jnp.float32)
        back = jnp.zeros((NX, NY, Z, GS), jnp.float32)
        for tap in range(27):
            back = back + shifted(dfield, tap, -1) * ker_f[tap]
        vol_grad = (grad.astype(jnp.float32) + back).astype(jnp.bfloat16)
        ker_grad = jnp.stack([lax.optimization_barrier(jnp.sum(shifted(vol_f, tap, 1) * dfield, axis=(0, 1, 2))) for tap in range(27)]) / scale
        mix_grad = jnp.dot(active.T, grad_rows, preferred_element_type=jnp.float32) / scale
        return (out.reshape(NX, NY, Z, GS), vol_grad, ker_grad, mix_grad)
    outs, vol_grads, ker_grads, mix_grads = lax.map(one_group, (vol_groups, ker_groups, mix_weight, gain_groups, grad_groups))
    output = jnp.moveaxis(outs, 0, 3).reshape(NX, NY, Z, C)
    volume_grad = jnp.moveaxis(vol_grads, 0, 3).reshape(NX, NY, Z, C)
    kernel_grad = jnp.moveaxis(ker_grads, 0, 1).reshape(27, C)
    return (output, volume_grad, kernel_grad, mix_grads)
```

```python
import jax
import jax.numpy as jnp
from jax import lax
from jax.sharding import PartitionSpec as P

SWEEPS = 5


HI = lax.Precision.HIGHEST
EPS = 1e-05


def padded_2(block, sides, width):
    for axis, dim in sides:
        count = lax.axis_size(axis)
        forward = [(i, i + 1) for i in range(count - 1)]
        forward.append((count - 1, 0))
        backward = [(target, source) for source, target in forward]
        low = lax.ppermute(
            lax.slice_in_dim(block, block.shape[dim] - width, None, axis=dim), axis, forward
        )
        high = lax.ppermute(lax.slice_in_dim(block, 0, width, axis=dim), axis, backward)
        block = jnp.concatenate([low, block, high], axis=dim)
    return block


BUTTERFLY = (("gx", 1), ("gx", 2), ("gx", 4), ("gx", 8), ("gx", 16), ("gx", 32), ("gy", 1), ("gy", 2))


def butterfly(value, combine):
    for axis, bit in BUTTERFLY:
        count = lax.axis_size(axis)
        if bit >= count:
            continue
        pairs = [(i, i ^ bit) for i in range(count)]
        value = combine(value, lax.ppermute(value, axis, pairs))
    return value


def butterfly_sum(parts):
    flat = jnp.concatenate([p.reshape(-1) for p in parts])
    flat = butterfly(flat, lambda a, b: a + b)
    out, start = [], 0
    for p in parts:
        out.append(flat[start : start + p.size].reshape(p.shape))
        start += p.size
    return out


def pack_moments(n, mean, scat):
    return jnp.concatenate([n.reshape(1), mean.reshape(-1), scat.reshape(-1)])


def unpack_moments(flat, groups, width):
    return (
        flat[0],
        flat[1 : 1 + groups * width].reshape(groups, width),
        flat[1 + groups * width :].reshape(groups, width, width),
    )


def merge_moments(a, b, groups, width):
    n_a, mean_a, scat_a = unpack_moments(a, groups, width)
    n_b, mean_b, scat_b = unpack_moments(b, groups, width)
    n = n_a + n_b
    mean = (n_a * mean_a + n_b * mean_b) / n
    delta = mean_b - mean_a
    outer = delta[:, :, None] * delta[:, None, :]
    scat = (scat_a + scat_b) + (n_a * n_b / n) * outer
    return pack_moments(n, mean, scat)


def whiten(sigma):
    eye = jnp.eye(sigma.shape[0], dtype=sigma.dtype)
    trace = jnp.trace(sigma)
    scaled = sigma / trace
    proj = eye
    for sweep in range(SWEEPS):
        cube = jnp.dot(
            proj, jnp.dot(proj, jnp.dot(proj, scaled, precision=HI), precision=HI), precision=HI
        )
        proj = 1.5 * proj - 0.5 * cube
    return proj / jnp.sqrt(trace)


def sigma_back(sigma, dwhite):
    return jax.vjp(whiten, sigma)[1](dwhite)[0]


def zwrap(field):
    return jnp.concatenate([field[:, :, -1:], field, field[:, :, :1]], axis=2)


def stencil(padded, kernel, flip):
    size_x, size_y, depth = (padded.shape[0] - 2, padded.shape[1] - 2, padded.shape[2] - 2)
    taps = kernel.astype(jnp.float32)
    total = jnp.zeros((size_x, size_y, depth, padded.shape[3]), jnp.float32)
    for tap in range(27):
        ox, oy, oz = (tap // 9, tap // 3 % 3, tap % 3)
        if flip:
            ox, oy, oz = (2 - ox, 2 - oy, 2 - oz)
        piece = padded[ox : ox + size_x, oy : oy + size_y, oz : oz + depth]
        total = total + piece.astype(jnp.float32) * taps[tap]
    return total


def inner(field, edge):
    return field[edge : field.shape[0] - edge, edge : field.shape[1] - edge]


def per_device(volume, void_mask, kernel, mix_weight, norm_gain, upstream):
    size_x, size_y, depth, chans = volume.shape
    groups, width = (mix_weight.shape[0], mix_weight.shape[1])
    scale = jnp.float32(size_x * size_y * depth * lax.axis_size("gx") * lax.axis_size("gy"))
    keep_own = (1 - void_mask).astype(jnp.float32)
    rim = 1
    padded_x = padded_2(volume, (("gx", 0), ("gy", 1)), 1)
    edge = rim - 1
    padded_z = zwrap(padded_x)
    field = lax.optimization_barrier(stencil(padded_z, kernel, False).astype(jnp.bfloat16)).astype(
        jnp.float32
    )
    ext_x, ext_y = (field.shape[0], field.shape[1])
    field_own = inner(field, edge)
    masked_own = keep_own[..., None] * field_own
    count_part = jnp.sum(keep_own)
    sum_part = jnp.sum(masked_own, axis=(0, 1, 2))
    eye = jnp.eye(width, dtype=jnp.float32)
    mean_part = (sum_part / count_part).reshape(groups, width)
    cent_part = field_own.reshape(size_x, size_y, depth, groups, width) - mean_part
    cov_part = jnp.einsum(
        "abzgi,abzgj->gij", keep_own[..., None, None] * cent_part, cent_part, precision=HI
    )
    moments = butterfly(
        pack_moments(count_part, mean_part, cov_part),
        lambda a, b: merge_moments(a, b, groups, width),
    )
    count, mean, scatter = unpack_moments(moments, groups, width)
    sigma = scatter / count + EPS * eye
    white = jax.vmap(whiten)(sigma)
    centered = field.reshape(ext_x, ext_y, depth, groups, width) - mean
    gain = norm_gain.reshape(groups, width)
    pre = jnp.einsum("abzgj,gij->abzgi", centered, white, precision=HI) * gain
    active = jax.nn.silu(pre).astype(jnp.bfloat16)
    active_own = inner(active, edge)
    grad_five = upstream.reshape(ext_x, ext_y, depth, groups, width)
    mixed = jnp.einsum(
        "abzgi,gio->abzgo", active_own, mix_weight, preferred_element_type=jnp.float32
    )
    output = (volume.astype(jnp.float32) + mixed.reshape(size_x, size_y, depth, chans)).astype(
        jnp.bfloat16
    )
    dact = jnp.einsum("abzgo,gio->abzgi", grad_five, mix_weight, preferred_element_type=jnp.float32)
    sig = jax.nn.sigmoid(pre)
    dnormed = dact * sig * (1.0 + pre * (1.0 - sig)) * gain
    dcent = jnp.einsum("abzgi,gij->abzgj", dnormed, white, precision=HI)
    dwhite_part = jnp.einsum(
        "abzgi,abzgj->gij", inner(dnormed, edge), inner(centered, edge), precision=HI
    )
    dsum_part = jnp.sum(inner(dcent, edge), axis=(0, 1, 2))
    dwhite, dsum = butterfly_sum((dwhite_part, dsum_part))
    sens = jax.vmap(sigma_back)(sigma, dwhite)
    sym = sens + jnp.swapaxes(sens, 1, 2)
    dfield = dcent + keep_own[..., None, None] / count * (
        jnp.einsum("abzgj,gjk->abzgk", centered, sym, precision=HI) - dsum
    )
    dfield = lax.optimization_barrier(
        dfield.astype(jnp.bfloat16).reshape(ext_x, ext_y, depth, chans)
    )
    dfield_pad = zwrap(padded_2(dfield, (("gx", 0), ("gy", 1)), 1))
    back = stencil(dfield_pad, kernel, True)
    volume_grad = (upstream.astype(jnp.float32) + back).astype(jnp.bfloat16)
    dfield_own = inner(dfield, edge).astype(jnp.float32)
    ker_terms = []
    for tap in range(27):
        ox, oy, oz = (tap // 9, tap // 3 % 3, tap % 3)
        piece = padded_z[
            edge + ox : edge + ox + size_x, edge + oy : edge + oy + size_y, oz : oz + depth
        ]
        ker_terms.append(jnp.sum(piece.astype(jnp.float32) * dfield_own, axis=(0, 1, 2)))
    ker_part = jnp.stack(ker_terms)
    mix_part = jnp.einsum(
        "abzgi,abzgo->gio",
        active_own,
        upstream.reshape(size_x, size_y, depth, groups, width),
        preferred_element_type=jnp.float32,
    )
    ker_sum, mix_sum = butterfly_sum((ker_part, mix_part))
    return (output, volume_grad, ker_sum / scale, mix_sum / scale)


def solution(mesh):
    in_specs = (
        P("gx", "gy", None, None),
        P("gx", "gy", None),
        P(),
        P(),
        P(),
        P("gx", "gy", None, None),
    )
    out_specs = (P("gx", "gy", None, None), P("gx", "gy", None, None), P(), P())
    return jax.shard_map(
        per_device, mesh=mesh, in_specs=in_specs, out_specs=out_specs, check_vma=False
    )
```

```python
import jax
import jax.numpy as jnp
from jax import lax
from jax.sharding import PartitionSpec as P

SWEEPS = 5


HI = lax.Precision.HIGHEST
EPS = 1e-05


def padded_2(block, sides, width):
    for axis, dim in sides:
        count = lax.axis_size(axis)
        forward = [(i, i + 1) for i in range(count - 1)]
        forward.append((count - 1, 0))
        backward = [(target, source) for source, target in forward]
        low = lax.ppermute(
            lax.slice_in_dim(block, block.shape[dim] - width, None, axis=dim), axis, forward
        )
        high = lax.ppermute(lax.slice_in_dim(block, 0, width, axis=dim), axis, backward)
        block = jnp.concatenate([low, block, high], axis=dim)
    return block


BUTTERFLY = (("gx", 1), ("gx", 2), ("gx", 4), ("gx", 8), ("gx", 16), ("gx", 32), ("gy", 1), ("gy", 2))


def butterfly(value, combine):
    for axis, bit in BUTTERFLY:
        count = lax.axis_size(axis)
        if bit >= count:
            continue
        pairs = [(i, i ^ bit) for i in range(count)]
        value = combine(value, lax.ppermute(value, axis, pairs))
    return value


def butterfly_sum(parts):
    rows = [p.reshape(-1, 128) for p in parts]
    flat = butterfly(jnp.concatenate(rows, axis=0), lambda a, b: a + b)
    out, start = [], 0
    for p, r in zip(parts, rows):
        out.append(flat[start : start + r.shape[0]].reshape(p.shape))
        start += r.shape[0]
    return out


def pack_moments(n, mean, scat):
    groups, width = mean.shape
    count = jnp.broadcast_to(n.reshape(1, 1, 1), (groups, 1, width))
    pad = jnp.zeros((groups, 6, width), jnp.float32)
    return jnp.concatenate([scat, mean[:, None, :], count, pad], axis=1)


def unpack_moments(packed):
    width = packed.shape[2]
    return (packed[:, width + 1 : width + 2], packed[:, width : width + 1], packed[:, :width])


def merge_moments(a, b):
    n_a, mean_a, scat_a = unpack_moments(a)
    n_b, mean_b, scat_b = unpack_moments(b)
    n = n_a + n_b
    mean = (n_a * mean_a + n_b * mean_b) / n
    delta = mean_b - mean_a
    outer = jnp.swapaxes(delta, 1, 2) * delta
    scat = (scat_a + scat_b) + (n_a * n_b / n) * outer
    pad = jnp.zeros_like(a[:, scat.shape[1] + 2 :])
    return jnp.concatenate([scat, mean, n, pad], axis=1)


def whiten(sigma):
    eye = jnp.eye(sigma.shape[0], dtype=sigma.dtype)
    trace = jnp.trace(sigma)
    scaled = sigma / trace
    proj = eye
    for sweep in range(SWEEPS):
        cube = jnp.dot(
            proj, jnp.dot(proj, jnp.dot(proj, scaled, precision=HI), precision=HI), precision=HI
        )
        proj = 1.5 * proj - 0.5 * cube
    return proj / jnp.sqrt(trace)


def sigma_back(sigma, dwhite):
    return jax.vjp(whiten, sigma)[1](dwhite)[0]


def zwrap(field):
    return jnp.concatenate([field[:, :, -1:], field, field[:, :, :1]], axis=2)


def stencil(padded, kernel, flip):
    size_x, size_y, depth = (padded.shape[0] - 2, padded.shape[1] - 2, padded.shape[2] - 2)
    taps = kernel.astype(jnp.float32)
    total = jnp.zeros((size_x, size_y, depth, padded.shape[3]), jnp.float32)
    for tap in range(27):
        ox, oy, oz = (tap // 9, tap // 3 % 3, tap % 3)
        if flip:
            ox, oy, oz = (2 - ox, 2 - oy, 2 - oz)
        piece = padded[ox : ox + size_x, oy : oy + size_y, oz : oz + depth]
        total = total + piece.astype(jnp.float32) * taps[tap]
    return total


def inner(field, edge):
    return field[edge : field.shape[0] - edge, edge : field.shape[1] - edge]


def per_device(volume, void_mask, kernel, mix_weight, norm_gain, upstream):
    size_x, size_y, depth, chans = volume.shape
    groups, width = (mix_weight.shape[0], mix_weight.shape[1])
    scale = jnp.float32(size_x * size_y * depth * lax.axis_size("gx") * lax.axis_size("gy"))
    keep_own = (1 - void_mask).astype(jnp.float32)
    rim = 1
    padded_x = padded_2(volume, (("gx", 0), ("gy", 1)), 1)
    edge = rim - 1
    padded_z = zwrap(padded_x)
    field = lax.optimization_barrier(stencil(padded_z, kernel, False).astype(jnp.bfloat16)).astype(
        jnp.float32
    )
    ext_x, ext_y = (field.shape[0], field.shape[1])
    field_own = inner(field, edge)
    masked_own = keep_own[..., None] * field_own
    count_part = jnp.sum(keep_own)
    sum_part = jnp.sum(masked_own, axis=(0, 1, 2))
    eye = jnp.eye(width, dtype=jnp.float32)
    mean_part = (sum_part / count_part).reshape(groups, width)
    cent_part = field_own.reshape(size_x, size_y, depth, groups, width) - mean_part
    cov_part = jnp.einsum(
        "abzgi,abzgj->gij", keep_own[..., None, None] * cent_part, cent_part, precision=HI
    )
    moments = butterfly(pack_moments(count_part, mean_part, cov_part), merge_moments)
    count, mean, scatter = unpack_moments(moments)
    count = count[0, 0, 0]
    mean = mean[:, 0]
    sigma = scatter / count + EPS * eye
    white = jax.vmap(whiten)(sigma)
    centered = field.reshape(ext_x, ext_y, depth, groups, width) - mean
    gain = norm_gain.reshape(groups, width)
    pre = jnp.einsum("abzgj,gij->abzgi", centered, white, precision=HI) * gain
    active = jax.nn.silu(pre).astype(jnp.bfloat16)
    active_own = inner(active, edge)
    grad_five = upstream.reshape(ext_x, ext_y, depth, groups, width)
    mixed = jnp.einsum(
        "abzgi,gio->abzgo", active_own, mix_weight, preferred_element_type=jnp.float32
    )
    output = (volume.astype(jnp.float32) + mixed.reshape(size_x, size_y, depth, chans)).astype(
        jnp.bfloat16
    )
    dact = jnp.einsum("abzgo,gio->abzgi", grad_five, mix_weight, preferred_element_type=jnp.float32)
    sig = jax.nn.sigmoid(pre)
    dnormed = dact * sig * (1.0 + pre * (1.0 - sig)) * gain
    dcent = jnp.einsum("abzgi,gij->abzgj", dnormed, white, precision=HI)
    dwhite_part = jnp.einsum(
        "abzgi,abzgj->gij", inner(dnormed, edge), inner(centered, edge), precision=HI
    )
    dsum_part = jnp.sum(inner(dcent, edge), axis=(0, 1, 2))
    dwhite, dsum = butterfly_sum((dwhite_part, dsum_part))
    sens = jax.vmap(sigma_back)(sigma, dwhite)
    sym = sens + jnp.swapaxes(sens, 1, 2)
    dfield = dcent + keep_own[..., None, None] / count * (
        jnp.einsum("abzgj,gjk->abzgk", centered, sym, precision=HI) - dsum
    )
    dfield = lax.optimization_barrier(
        dfield.astype(jnp.bfloat16).reshape(ext_x, ext_y, depth, chans)
    )
    dfield_pad = zwrap(padded_2(dfield, (("gx", 0), ("gy", 1)), 1))
    back = stencil(dfield_pad, kernel, True)
    volume_grad = (upstream.astype(jnp.float32) + back).astype(jnp.bfloat16)
    dfield_own = inner(dfield, edge).astype(jnp.float32)
    ker_terms = []
    for tap in range(27):
        ox, oy, oz = (tap // 9, tap // 3 % 3, tap % 3)
        piece = padded_z[
            edge + ox : edge + ox + size_x, edge + oy : edge + oy + size_y, oz : oz + depth
        ]
        ker_terms.append(jnp.sum(piece.astype(jnp.float32) * dfield_own, axis=(0, 1, 2)))
    ker_part = jnp.stack(ker_terms)
    mix_part = jnp.einsum(
        "abzgi,abzgo->gio",
        active_own,
        upstream.reshape(size_x, size_y, depth, groups, width),
        preferred_element_type=jnp.float32,
    )
    ker_sum, mix_sum = butterfly_sum((ker_part, mix_part))
    return (output, volume_grad, ker_sum / scale, mix_sum / scale)


def solution(mesh):
    in_specs = (
        P("gx", "gy", None, None),
        P("gx", "gy", None),
        P(),
        P(),
        P(),
        P("gx", "gy", None, None),
    )
    out_specs = (P("gx", "gy", None, None), P("gx", "gy", None, None), P(), P())
    return jax.shard_map(
        per_device, mesh=mesh, in_specs=in_specs, out_specs=out_specs, check_vma=False
    )
```

```python
import jax
import jax.numpy as jnp
from jax import lax
from jax.experimental import pallas as pl
from jax.sharding import PartitionSpec as P

SWEEPS = 5


HI = lax.Precision.HIGHEST
EPS = 1e-05


def padded_2(block, sides, width):
    for axis, dim in sides:
        count = lax.axis_size(axis)
        forward = [(i, i + 1) for i in range(count - 1)]
        forward.append((count - 1, 0))
        backward = [(target, source) for source, target in forward]
        low = lax.ppermute(
            lax.slice_in_dim(block, block.shape[dim] - width, None, axis=dim), axis, forward
        )
        high = lax.ppermute(lax.slice_in_dim(block, 0, width, axis=dim), axis, backward)
        block = jnp.concatenate([low, block, high], axis=dim)
    return block


BUTTERFLY = (("gx", 1), ("gx", 2), ("gx", 4), ("gx", 8), ("gx", 16), ("gx", 32), ("gy", 1), ("gy", 2))


def butterfly(value, combine):
    for axis, bit in BUTTERFLY:
        count = lax.axis_size(axis)
        if bit >= count:
            continue
        pairs = [(i, i ^ bit) for i in range(count)]
        value = combine(value, lax.ppermute(value, axis, pairs))
    return value


def butterfly_sum(parts):
    rows = [p.reshape(-1, 128) for p in parts]
    flat = butterfly(jnp.concatenate(rows, axis=0), lambda a, b: a + b)
    out, start = [], 0
    for p, r in zip(parts, rows):
        out.append(flat[start : start + r.shape[0]].reshape(p.shape))
        start += r.shape[0]
    return out


def pack_moments(n, mean, scat):
    groups, width = mean.shape
    count = jnp.broadcast_to(n.reshape(1, 1, 1), (groups, 1, width))
    pad = jnp.zeros((groups, 6, width), jnp.float32)
    return jnp.concatenate([scat, mean[:, None, :], count, pad], axis=1)


def unpack_moments(packed):
    width = packed.shape[2]
    return (packed[:, width + 1 : width + 2], packed[:, width : width + 1], packed[:, :width])


def merge_moments(a, b):
    n_a, mean_a, scat_a = unpack_moments(a)
    n_b, mean_b, scat_b = unpack_moments(b)
    n = n_a + n_b
    mean = (n_a * mean_a + n_b * mean_b) / n
    delta = mean_b - mean_a
    outer = jnp.swapaxes(delta, 1, 2) * delta
    scat = (scat_a + scat_b) + (n_a * n_b / n) * outer
    pad = jnp.zeros_like(a[:, scat.shape[1] + 2 :])
    return jnp.concatenate([scat, mean, n, pad], axis=1)


def whiten(sigma):
    eye = jnp.eye(sigma.shape[0], dtype=sigma.dtype)
    trace = jnp.trace(sigma)
    scaled = sigma / trace
    proj = eye
    for sweep in range(SWEEPS):
        cube = jnp.dot(
            proj, jnp.dot(proj, jnp.dot(proj, scaled, precision=HI), precision=HI), precision=HI
        )
        proj = 1.5 * proj - 0.5 * cube
    return proj / jnp.sqrt(trace)


def mm(a, b):
    return jnp.dot(a, b, precision=HI, preferred_element_type=jnp.float32)


def unit(width):
    rows = lax.broadcasted_iota(jnp.int32, (width, width), 0)
    cols = lax.broadcasted_iota(jnp.int32, (width, width), 1)
    return (rows == cols).astype(jnp.float32)


def whiten_fwd_kernel(sig_ref, white_ref, scaled_ref, ps_ref, as_ref, bs_ref):
    sig = sig_ref[...]
    eye = unit(sig.shape[0])
    trace = jnp.sum(sig * eye, keepdims=True)
    scaled = sig / trace
    scaled_ref[...] = scaled
    proj = eye
    for sweep in range(SWEEPS):
        ps_ref[sweep] = proj
        first = mm(proj, scaled)
        as_ref[sweep] = first
        second = mm(proj, first)
        bs_ref[sweep] = second
        proj = 1.5 * proj - 0.5 * mm(proj, second)
    ps_ref[SWEEPS] = proj
    white_ref[...] = proj / jnp.sqrt(trace)


def whiten_bwd_kernel(sig_ref, scaled_ref, ps_ref, as_ref, bs_ref, dwhite_ref, sens_ref):
    sig = sig_ref[...]
    eye = unit(sig.shape[0])
    trace = jnp.sum(sig * eye, keepdims=True)
    root = jnp.sqrt(trace)
    dwhite = dwhite_ref[...]
    scaled = scaled_ref[...]
    grad = dwhite / root
    grad_trace = -0.5 * jnp.sum(dwhite * ps_ref[SWEEPS], keepdims=True) / (trace * root)
    grad_scaled = jnp.zeros_like(sig)
    for sweep in reversed(range(SWEEPS)):
        proj = ps_ref[sweep]
        grad_cube = -0.5 * grad
        grad_second = mm(proj, grad_cube)
        grad_first = mm(proj, grad_second)
        grad_scaled = grad_scaled + mm(proj, grad_first)
        grad = (
            1.5 * grad
            + mm(grad_cube, bs_ref[sweep])
            + mm(grad_second, as_ref[sweep])
            + mm(grad_first, scaled)
        )
    grad_trace = grad_trace - jnp.sum(grad_scaled * sig, keepdims=True) / (trace * trace)
    sens_ref[...] = grad_scaled / trace + grad_trace * eye


def whiten_fwd(sigma):
    groups, width, _ = sigma.shape
    mat = pl.BlockSpec((None, width, width), lambda g: (g, 0, 0))
    stack = lambda n: pl.BlockSpec((None, n, width, width), lambda g: (g, 0, 0, 0))
    f32 = jnp.float32
    return pl.pallas_call(
        whiten_fwd_kernel,
        grid=(groups,),
        in_specs=[mat],
        out_specs=[mat, mat, stack(SWEEPS + 1), stack(SWEEPS), stack(SWEEPS)],
        out_shape=[
            jax.ShapeDtypeStruct((groups, width, width), f32),
            jax.ShapeDtypeStruct((groups, width, width), f32),
            jax.ShapeDtypeStruct((groups, SWEEPS + 1, width, width), f32),
            jax.ShapeDtypeStruct((groups, SWEEPS, width, width), f32),
            jax.ShapeDtypeStruct((groups, SWEEPS, width, width), f32),
        ],
    )(sigma)


def whiten_bwd(sigma, scaled, ps, as_, bs, dwhite):
    groups, width, _ = sigma.shape
    mat = pl.BlockSpec((None, width, width), lambda g: (g, 0, 0))
    stack = lambda n: pl.BlockSpec((None, n, width, width), lambda g: (g, 0, 0, 0))
    return pl.pallas_call(
        whiten_bwd_kernel,
        grid=(groups,),
        in_specs=[mat, mat, stack(SWEEPS + 1), stack(SWEEPS), stack(SWEEPS), mat],
        out_specs=mat,
        out_shape=jax.ShapeDtypeStruct((groups, width, width), jnp.float32),
    )(sigma, scaled, ps, as_, bs, dwhite)


def zwrap(field):
    return jnp.concatenate([field[:, :, -1:], field, field[:, :, :1]], axis=2)


def stencil(padded, kernel, flip):
    size_x, size_y, depth = (padded.shape[0] - 2, padded.shape[1] - 2, padded.shape[2] - 2)
    taps = kernel.astype(jnp.float32)
    total = jnp.zeros((size_x, size_y, depth, padded.shape[3]), jnp.float32)
    for tap in range(27):
        ox, oy, oz = (tap // 9, tap // 3 % 3, tap % 3)
        if flip:
            ox, oy, oz = (2 - ox, 2 - oy, 2 - oz)
        piece = padded[ox : ox + size_x, oy : oy + size_y, oz : oz + depth]
        total = total + piece.astype(jnp.float32) * taps[tap]
    return total


def inner(field, edge):
    return field[edge : field.shape[0] - edge, edge : field.shape[1] - edge]


def per_device(volume, void_mask, kernel, mix_weight, norm_gain, upstream):
    size_x, size_y, depth, chans = volume.shape
    groups, width = (mix_weight.shape[0], mix_weight.shape[1])
    scale = jnp.float32(size_x * size_y * depth * lax.axis_size("gx") * lax.axis_size("gy"))
    keep_own = (1 - void_mask).astype(jnp.float32)
    rim = 1
    padded_x = padded_2(volume, (("gx", 0), ("gy", 1)), 1)
    edge = rim - 1
    padded_z = zwrap(padded_x)
    field = lax.optimization_barrier(stencil(padded_z, kernel, False).astype(jnp.bfloat16)).astype(
        jnp.float32
    )
    ext_x, ext_y = (field.shape[0], field.shape[1])
    field_own = inner(field, edge)
    masked_own = keep_own[..., None] * field_own
    count_part = jnp.sum(keep_own)
    sum_part = jnp.sum(masked_own, axis=(0, 1, 2))
    eye = jnp.eye(width, dtype=jnp.float32)
    mean_part = (sum_part / count_part).reshape(groups, width)
    cent_part = field_own.reshape(size_x, size_y, depth, groups, width) - mean_part
    cov_part = jnp.einsum(
        "abzgi,abzgj->gij", keep_own[..., None, None] * cent_part, cent_part, precision=HI
    )
    moments = butterfly(pack_moments(count_part, mean_part, cov_part), merge_moments)
    count, mean, scatter = unpack_moments(moments)
    count = count[0, 0, 0]
    mean = mean[:, 0]
    sigma = scatter / count + EPS * eye
    white, scaled, ps, as_, bs = whiten_fwd(sigma)
    centered = field.reshape(ext_x, ext_y, depth, groups, width) - mean
    gain = norm_gain.reshape(groups, width)
    pre = jnp.einsum("abzgj,gij->abzgi", centered, white, precision=HI) * gain
    active = jax.nn.silu(pre).astype(jnp.bfloat16)
    active_own = inner(active, edge)
    grad_five = upstream.reshape(ext_x, ext_y, depth, groups, width)
    mixed = jnp.einsum(
        "abzgi,gio->abzgo", active_own, mix_weight, preferred_element_type=jnp.float32
    )
    output = (volume.astype(jnp.float32) + mixed.reshape(size_x, size_y, depth, chans)).astype(
        jnp.bfloat16
    )
    dact = jnp.einsum("abzgo,gio->abzgi", grad_five, mix_weight, preferred_element_type=jnp.float32)
    sig = jax.nn.sigmoid(pre)
    dnormed = dact * sig * (1.0 + pre * (1.0 - sig)) * gain
    dcent = jnp.einsum("abzgi,gij->abzgj", dnormed, white, precision=HI)
    dwhite_part = jnp.einsum(
        "abzgi,abzgj->gij", inner(dnormed, edge), inner(centered, edge), precision=HI
    )
    dsum_part = jnp.sum(inner(dcent, edge), axis=(0, 1, 2))
    dwhite, dsum = butterfly_sum((dwhite_part, dsum_part))
    sens = whiten_bwd(sigma, scaled, ps, as_, bs, dwhite)
    sym = sens + jnp.swapaxes(sens, 1, 2)
    dfield = dcent + keep_own[..., None, None] / count * (
        jnp.einsum("abzgj,gjk->abzgk", centered, sym, precision=HI) - dsum
    )
    dfield = lax.optimization_barrier(
        dfield.astype(jnp.bfloat16).reshape(ext_x, ext_y, depth, chans)
    )
    dfield_pad = zwrap(padded_2(dfield, (("gx", 0), ("gy", 1)), 1))
    back = stencil(dfield_pad, kernel, True)
    volume_grad = (upstream.astype(jnp.float32) + back).astype(jnp.bfloat16)
    dfield_own = inner(dfield, edge).astype(jnp.float32)
    ker_terms = []
    for tap in range(27):
        ox, oy, oz = (tap // 9, tap // 3 % 3, tap % 3)
        piece = padded_z[
            edge + ox : edge + ox + size_x, edge + oy : edge + oy + size_y, oz : oz + depth
        ]
        ker_terms.append(jnp.sum(piece.astype(jnp.float32) * dfield_own, axis=(0, 1, 2)))
    ker_part = jnp.stack(ker_terms)
    mix_part = jnp.einsum(
        "abzgi,abzgo->gio",
        active_own,
        upstream.reshape(size_x, size_y, depth, groups, width),
        preferred_element_type=jnp.float32,
    )
    ker_sum, mix_sum = butterfly_sum((ker_part, mix_part))
    return (output, volume_grad, ker_sum / scale, mix_sum / scale)


def solution(mesh):
    in_specs = (
        P("gx", "gy", None, None),
        P("gx", "gy", None),
        P(),
        P(),
        P(),
        P("gx", "gy", None, None),
    )
    out_specs = (P("gx", "gy", None, None), P("gx", "gy", None, None), P(), P())
    return jax.shard_map(
        per_device, mesh=mesh, in_specs=in_specs, out_specs=out_specs, check_vma=False
    )
```

```python
import jax
import jax.numpy as jnp
from jax import lax
from jax.experimental import pallas as pl
from jax.sharding import PartitionSpec as P

SWEEPS = 5


HI = lax.Precision.HIGHEST
EPS = 1e-05


def padded_2(block, sides, width):
    for axis, dim in sides:
        count = lax.axis_size(axis)
        forward = [(i, i + 1) for i in range(count - 1)]
        forward.append((count - 1, 0))
        backward = [(target, source) for source, target in forward]
        low = lax.ppermute(
            lax.slice_in_dim(block, block.shape[dim] - width, None, axis=dim), axis, forward
        )
        high = lax.ppermute(lax.slice_in_dim(block, 0, width, axis=dim), axis, backward)
        block = jnp.concatenate([low, block, high], axis=dim)
    return block


BUTTERFLY = (("gx", 1), ("gx", 2), ("gx", 4), ("gx", 8), ("gx", 16), ("gx", 32), ("gy", 1), ("gy", 2))


def butterfly(value, combine):
    for axis, bit in BUTTERFLY:
        count = lax.axis_size(axis)
        if bit >= count:
            continue
        pairs = [(i, i ^ bit) for i in range(count)]
        value = combine(value, lax.ppermute(value, axis, pairs))
    return value


def butterfly_sum(parts):
    rows = [p.reshape(-1, 128) for p in parts]
    flat = butterfly(jnp.concatenate(rows, axis=0), lambda a, b: a + b)
    out, start = [], 0
    for p, r in zip(parts, rows):
        out.append(flat[start : start + r.shape[0]].reshape(p.shape))
        start += r.shape[0]
    return out


def pack_moments(n, mean, scat):
    groups, width = mean.shape
    count = jnp.broadcast_to(n.reshape(1, 1, 1), (groups, 1, width))
    pad = jnp.zeros((groups, 6, width), jnp.float32)
    return jnp.concatenate([scat, mean[:, None, :], count, pad], axis=1)


def unpack_moments(packed):
    width = packed.shape[2]
    return (packed[:, width + 1 : width + 2], packed[:, width : width + 1], packed[:, :width])


def merge_moments(a, b):
    n_a, mean_a, scat_a = unpack_moments(a)
    n_b, mean_b, scat_b = unpack_moments(b)
    n = n_a + n_b
    mean = (n_a * mean_a + n_b * mean_b) / n
    delta = mean_b - mean_a
    outer = jnp.swapaxes(delta, 1, 2) * delta
    scat = (scat_a + scat_b) + (n_a * n_b / n) * outer
    pad = jnp.zeros_like(a[:, scat.shape[1] + 2 :])
    return jnp.concatenate([scat, mean, n, pad], axis=1)


def whiten(sigma):
    eye = jnp.eye(sigma.shape[0], dtype=sigma.dtype)
    trace = jnp.trace(sigma)
    scaled = sigma / trace
    proj = eye
    for sweep in range(SWEEPS):
        cube = jnp.dot(
            proj, jnp.dot(proj, jnp.dot(proj, scaled, precision=HI), precision=HI), precision=HI
        )
        proj = 1.5 * proj - 0.5 * cube
    return proj / jnp.sqrt(trace)


def mm(a, b):
    return jnp.dot(a, b, precision=HI, preferred_element_type=jnp.float32)


def unit(width):
    rows = lax.broadcasted_iota(jnp.int32, (width, width), 0)
    cols = lax.broadcasted_iota(jnp.int32, (width, width), 1)
    return (rows == cols).astype(jnp.float32)


def whiten_fwd_kernel(sig_ref, white_ref, scaled_ref, ps_ref, as_ref, bs_ref):
    groups, width, _ = sig_ref.shape
    eye = unit(width)
    traces, scaled, proj = [], [], []
    for g in range(groups):
        sig = sig_ref[g]
        trace = jnp.sum(sig * eye, keepdims=True)
        traces.append(trace)
        scaled.append(sig / trace)
        scaled_ref[g] = scaled[g]
        proj.append(eye)
    for sweep in range(SWEEPS):
        first = [mm(proj[g], scaled[g]) for g in range(groups)]
        second = [mm(proj[g], first[g]) for g in range(groups)]
        cube = [mm(proj[g], second[g]) for g in range(groups)]
        for g in range(groups):
            ps_ref[g, sweep] = proj[g]
            as_ref[g, sweep] = first[g]
            bs_ref[g, sweep] = second[g]
            proj[g] = 1.5 * proj[g] - 0.5 * cube[g]
    for g in range(groups):
        ps_ref[g, SWEEPS] = proj[g]
        white_ref[g] = proj[g] / jnp.sqrt(traces[g])


def whiten_bwd_kernel(sig_ref, scaled_ref, ps_ref, as_ref, bs_ref, dwhite_ref, sens_ref):
    groups, width, _ = sig_ref.shape
    eye = unit(width)
    traces, roots, grad, grad_trace, grad_scaled = [], [], [], [], []
    for g in range(groups):
        sig = sig_ref[g]
        trace = jnp.sum(sig * eye, keepdims=True)
        root = jnp.sqrt(trace)
        dwhite = dwhite_ref[g]
        traces.append(trace)
        grad.append(dwhite / root)
        grad_trace.append(-0.5 * jnp.sum(dwhite * ps_ref[g, SWEEPS], keepdims=True) / (trace * root))
        grad_scaled.append(jnp.zeros_like(sig))
    for sweep in reversed(range(SWEEPS)):
        proj = [ps_ref[g, sweep] for g in range(groups)]
        grad_cube = [-0.5 * grad[g] for g in range(groups)]
        grad_second = [mm(proj[g], grad_cube[g]) for g in range(groups)]
        grad_first = [mm(proj[g], grad_second[g]) for g in range(groups)]
        for g in range(groups):
            grad_scaled[g] = grad_scaled[g] + mm(proj[g], grad_first[g])
            grad[g] = (
                1.5 * grad[g]
                + mm(grad_cube[g], bs_ref[g, sweep])
                + mm(grad_second[g], as_ref[g, sweep])
                + mm(grad_first[g], scaled_ref[g])
            )
    for g in range(groups):
        trace = traces[g]
        total = grad_trace[g] - jnp.sum(grad_scaled[g] * sig_ref[g], keepdims=True) / (trace * trace)
        sens_ref[g] = grad_scaled[g] / trace + total * eye


def whiten_fwd(sigma):
    groups, width, _ = sigma.shape
    f32 = jnp.float32
    return pl.pallas_call(
        whiten_fwd_kernel,
        out_shape=[
            jax.ShapeDtypeStruct((groups, width, width), f32),
            jax.ShapeDtypeStruct((groups, width, width), f32),
            jax.ShapeDtypeStruct((groups, SWEEPS + 1, width, width), f32),
            jax.ShapeDtypeStruct((groups, SWEEPS, width, width), f32),
            jax.ShapeDtypeStruct((groups, SWEEPS, width, width), f32),
        ],
    )(sigma)


def whiten_bwd(sigma, scaled, ps, as_, bs, dwhite):
    groups, width, _ = sigma.shape
    return pl.pallas_call(
        whiten_bwd_kernel,
        out_shape=jax.ShapeDtypeStruct((groups, width, width), jnp.float32),
    )(sigma, scaled, ps, as_, bs, dwhite)


def zwrap(field):
    return jnp.concatenate([field[:, :, -1:], field, field[:, :, :1]], axis=2)


def stencil(padded, kernel, flip):
    size_x, size_y, depth = (padded.shape[0] - 2, padded.shape[1] - 2, padded.shape[2] - 2)
    taps = kernel.astype(jnp.float32)
    total = jnp.zeros((size_x, size_y, depth, padded.shape[3]), jnp.float32)
    for tap in range(27):
        ox, oy, oz = (tap // 9, tap // 3 % 3, tap % 3)
        if flip:
            ox, oy, oz = (2 - ox, 2 - oy, 2 - oz)
        piece = padded[ox : ox + size_x, oy : oy + size_y, oz : oz + depth]
        total = total + piece.astype(jnp.float32) * taps[tap]
    return total


def inner(field, edge):
    return field[edge : field.shape[0] - edge, edge : field.shape[1] - edge]


def per_device(volume, void_mask, kernel, mix_weight, norm_gain, upstream):
    size_x, size_y, depth, chans = volume.shape
    groups, width = (mix_weight.shape[0], mix_weight.shape[1])
    scale = jnp.float32(size_x * size_y * depth * lax.axis_size("gx") * lax.axis_size("gy"))
    keep_own = (1 - void_mask).astype(jnp.float32)
    rim = 1
    padded_x = padded_2(volume, (("gx", 0), ("gy", 1)), 1)
    edge = rim - 1
    padded_z = zwrap(padded_x)
    field = lax.optimization_barrier(stencil(padded_z, kernel, False).astype(jnp.bfloat16)).astype(
        jnp.float32
    )
    ext_x, ext_y = (field.shape[0], field.shape[1])
    field_own = inner(field, edge)
    masked_own = keep_own[..., None] * field_own
    count_part = jnp.sum(keep_own)
    sum_part = jnp.sum(masked_own, axis=(0, 1, 2))
    eye = jnp.eye(width, dtype=jnp.float32)
    mean_part = (sum_part / count_part).reshape(groups, width)
    cent_part = field_own.reshape(size_x, size_y, depth, groups, width) - mean_part
    cov_part = jnp.einsum(
        "abzgi,abzgj->gij", keep_own[..., None, None] * cent_part, cent_part, precision=HI
    )
    moments = butterfly(pack_moments(count_part, mean_part, cov_part), merge_moments)
    count, mean, scatter = unpack_moments(moments)
    count = count[0, 0, 0]
    mean = mean[:, 0]
    sigma = scatter / count + EPS * eye
    white, scaled, ps, as_, bs = whiten_fwd(sigma)
    centered = field.reshape(ext_x, ext_y, depth, groups, width) - mean
    gain = norm_gain.reshape(groups, width)
    pre = jnp.einsum("abzgj,gij->abzgi", centered, white, precision=HI) * gain
    active = jax.nn.silu(pre).astype(jnp.bfloat16)
    active_own = inner(active, edge)
    grad_five = upstream.reshape(ext_x, ext_y, depth, groups, width)
    mixed = jnp.einsum(
        "abzgi,gio->abzgo", active_own, mix_weight, preferred_element_type=jnp.float32
    )
    output = (volume.astype(jnp.float32) + mixed.reshape(size_x, size_y, depth, chans)).astype(
        jnp.bfloat16
    )
    mix_part = jnp.einsum(
        "abzgi,abzgo->gio",
        active_own,
        upstream.reshape(size_x, size_y, depth, groups, width),
        preferred_element_type=jnp.float32,
    )
    (mix_sum,) = butterfly_sum((mix_part,))
    dact = jnp.einsum("abzgo,gio->abzgi", grad_five, mix_weight, preferred_element_type=jnp.float32)
    sig = jax.nn.sigmoid(pre)
    dnormed = dact * sig * (1.0 + pre * (1.0 - sig)) * gain
    dcent = jnp.einsum("abzgi,gij->abzgj", dnormed, white, precision=HI)
    dwhite_part = jnp.einsum(
        "abzgi,abzgj->gij", inner(dnormed, edge), inner(centered, edge), precision=HI
    )
    dsum_part = jnp.sum(inner(dcent, edge), axis=(0, 1, 2))
    dwhite, dsum = butterfly_sum((dwhite_part, dsum_part))
    sens = whiten_bwd(sigma, scaled, ps, as_, bs, dwhite)
    sym = sens + jnp.swapaxes(sens, 1, 2)
    dfield = dcent + keep_own[..., None, None] / count * (
        jnp.einsum("abzgj,gjk->abzgk", centered, sym, precision=HI) - dsum
    )
    dfield = lax.optimization_barrier(
        dfield.astype(jnp.bfloat16).reshape(ext_x, ext_y, depth, chans)
    )
    dfield_pad = zwrap(padded_2(dfield, (("gx", 0), ("gy", 1)), 1))
    back = stencil(dfield_pad, kernel, True)
    volume_grad = (upstream.astype(jnp.float32) + back).astype(jnp.bfloat16)
    dfield_own = inner(dfield, edge).astype(jnp.float32)
    ker_terms = []
    for tap in range(27):
        ox, oy, oz = (tap // 9, tap // 3 % 3, tap % 3)
        piece = padded_z[
            edge + ox : edge + ox + size_x, edge + oy : edge + oy + size_y, oz : oz + depth
        ]
        ker_terms.append(jnp.sum(piece.astype(jnp.float32) * dfield_own, axis=(0, 1, 2)))
    ker_part = jnp.stack(ker_terms)
    (ker_sum,) = butterfly_sum((ker_part,))
    return (output, volume_grad, ker_sum / scale, mix_sum / scale)


def solution(mesh):
    in_specs = (
        P("gx", "gy", None, None),
        P("gx", "gy", None),
        P(),
        P(),
        P(),
        P("gx", "gy", None, None),
    )
    out_specs = (P("gx", "gy", None, None), P("gx", "gy", None, None), P(), P())
    return jax.shard_map(
        per_device, mesh=mesh, in_specs=in_specs, out_specs=out_specs, check_vma=False
    )
```

```python
import jax
import jax.numpy as jnp
from jax import lax
from jax.experimental import pallas as pl
from jax.sharding import PartitionSpec as P

SWEEPS = 5


HI = lax.Precision.HIGHEST
EPS = 1e-05


def halo_2d(block):
    nx, ny = (lax.axis_size("gx"), lax.axis_size("gy"))
    spans = {-1: slice(-1, None), 0: slice(None), 1: slice(0, 1)}
    pieces = {(0, 0): block}
    for dx in (-1, 0, 1):
        for dy in (-1, 0, 1):
            if dx == 0 and dy == 0:
                continue
            pairs = [
                (ix * ny + iy, (ix - dx) % nx * ny + (iy - dy) % ny)
                for ix in range(nx)
                for iy in range(ny)
            ]
            piece = block[spans[dx], spans[dy]]
            pieces[dx, dy] = lax.ppermute(piece, ("gx", "gy"), pairs)
    rows = [jnp.concatenate([pieces[dx, dy] for dy in (-1, 0, 1)], axis=1) for dx in (-1, 0, 1)]
    return jnp.concatenate(rows, axis=0)


BUTTERFLY = (("gx", 1), ("gx", 2), ("gx", 4), ("gx", 8), ("gx", 16), ("gx", 32), ("gy", 1), ("gy", 2))


def butterfly(value, combine):
    for axis, bit in BUTTERFLY:
        count = lax.axis_size(axis)
        if bit >= count:
            continue
        pairs = [(i, i ^ bit) for i in range(count)]
        value = combine(value, lax.ppermute(value, axis, pairs))
    return value


def butterfly_sum(parts):
    rows = [p.reshape(-1, 128) for p in parts]
    flat = butterfly(jnp.concatenate(rows, axis=0), lambda a, b: a + b)
    out, start = [], 0
    for p, r in zip(parts, rows):
        out.append(flat[start : start + r.shape[0]].reshape(p.shape))
        start += r.shape[0]
    return out


def pack_moments(n, mean, scat):
    groups, width = mean.shape
    count = jnp.broadcast_to(n.reshape(1, 1, 1), (groups, 1, width))
    pad = jnp.zeros((groups, 6, width), jnp.float32)
    return jnp.concatenate([scat, mean[:, None, :], count, pad], axis=1)


def unpack_moments(packed):
    width = packed.shape[2]
    return (packed[:, width + 1 : width + 2], packed[:, width : width + 1], packed[:, :width])


def merge_moments(a, b):
    n_a, mean_a, scat_a = unpack_moments(a)
    n_b, mean_b, scat_b = unpack_moments(b)
    n = n_a + n_b
    mean = (n_a * mean_a + n_b * mean_b) / n
    delta = mean_b - mean_a
    outer = jnp.swapaxes(delta, 1, 2) * delta
    scat = (scat_a + scat_b) + (n_a * n_b / n) * outer
    pad = jnp.zeros_like(a[:, scat.shape[1] + 2 :])
    return jnp.concatenate([scat, mean, n, pad], axis=1)


def whiten(sigma):
    eye = jnp.eye(sigma.shape[0], dtype=sigma.dtype)
    trace = jnp.trace(sigma)
    scaled = sigma / trace
    proj = eye
    for sweep in range(SWEEPS):
        cube = jnp.dot(
            proj, jnp.dot(proj, jnp.dot(proj, scaled, precision=HI), precision=HI), precision=HI
        )
        proj = 1.5 * proj - 0.5 * cube
    return proj / jnp.sqrt(trace)


def mm(a, b):
    return jnp.dot(a, b, precision=HI, preferred_element_type=jnp.float32)


def unit(width):
    rows = lax.broadcasted_iota(jnp.int32, (width, width), 0)
    cols = lax.broadcasted_iota(jnp.int32, (width, width), 1)
    return (rows == cols).astype(jnp.float32)


def whiten_fwd_kernel(sig_ref, white_ref, scaled_ref, ps_ref, as_ref, bs_ref):
    groups, width, _ = sig_ref.shape
    eye = unit(width)
    traces, scaled, proj = [], [], []
    for g in range(groups):
        sig = sig_ref[g]
        trace = jnp.sum(sig * eye, keepdims=True)
        traces.append(trace)
        scaled.append(sig / trace)
        scaled_ref[g] = scaled[g]
        proj.append(eye)

    def sweep_step(sweep, proj):
        first = [mm(proj[g], scaled[g]) for g in range(groups)]
        second = [mm(proj[g], first[g]) for g in range(groups)]
        cube = [mm(proj[g], second[g]) for g in range(groups)]
        for g in range(groups):
            ps_ref[g, sweep] = proj[g]
            as_ref[g, sweep] = first[g]
            bs_ref[g, sweep] = second[g]
        return [1.5 * proj[g] - 0.5 * cube[g] for g in range(groups)]

    proj = lax.fori_loop(0, SWEEPS, sweep_step, proj)
    for g in range(groups):
        ps_ref[g, SWEEPS] = proj[g]
        white_ref[g] = proj[g] / jnp.sqrt(traces[g])


def whiten_bwd_kernel(sig_ref, scaled_ref, ps_ref, as_ref, bs_ref, dwhite_ref, sens_ref):
    groups, width, _ = sig_ref.shape
    eye = unit(width)
    traces, roots, grad, grad_trace, grad_scaled = [], [], [], [], []
    for g in range(groups):
        sig = sig_ref[g]
        trace = jnp.sum(sig * eye, keepdims=True)
        root = jnp.sqrt(trace)
        dwhite = dwhite_ref[g]
        traces.append(trace)
        grad.append(dwhite / root)
        grad_trace.append(-0.5 * jnp.sum(dwhite * ps_ref[g, SWEEPS], keepdims=True) / (trace * root))
        grad_scaled.append(jnp.zeros_like(sig))

    def sweep_step(step, carry):
        grad, grad_scaled = carry
        sweep = SWEEPS - 1 - step
        proj = [ps_ref[g, sweep] for g in range(groups)]
        grad_cube = [-0.5 * grad[g] for g in range(groups)]
        grad_second = [mm(proj[g], grad_cube[g]) for g in range(groups)]
        grad_first = [mm(proj[g], grad_second[g]) for g in range(groups)]
        new_scaled, new_grad = [], []
        for g in range(groups):
            new_scaled.append(grad_scaled[g] + mm(proj[g], grad_first[g]))
            new_grad.append(
                1.5 * grad[g]
                + mm(grad_cube[g], bs_ref[g, sweep])
                + mm(grad_second[g], as_ref[g, sweep])
                + mm(grad_first[g], scaled_ref[g])
            )
        return (new_grad, new_scaled)

    grad, grad_scaled = lax.fori_loop(0, SWEEPS, sweep_step, (grad, grad_scaled))
    for g in range(groups):
        trace = traces[g]
        total = grad_trace[g] - jnp.sum(grad_scaled[g] * sig_ref[g], keepdims=True) / (trace * trace)
        sens_ref[g] = grad_scaled[g] / trace + total * eye


def whiten_fwd(sigma):
    groups, width, _ = sigma.shape
    f32 = jnp.float32
    return pl.pallas_call(
        whiten_fwd_kernel,
        out_shape=[
            jax.ShapeDtypeStruct((groups, width, width), f32),
            jax.ShapeDtypeStruct((groups, width, width), f32),
            jax.ShapeDtypeStruct((groups, SWEEPS + 1, width, width), f32),
            jax.ShapeDtypeStruct((groups, SWEEPS, width, width), f32),
            jax.ShapeDtypeStruct((groups, SWEEPS, width, width), f32),
        ],
    )(sigma)


def whiten_bwd(sigma, scaled, ps, as_, bs, dwhite):
    groups, width, _ = sigma.shape
    return pl.pallas_call(
        whiten_bwd_kernel,
        out_shape=jax.ShapeDtypeStruct((groups, width, width), jnp.float32),
    )(sigma, scaled, ps, as_, bs, dwhite)


def zwrap(field):
    return jnp.concatenate([field[:, :, -1:], field, field[:, :, :1]], axis=2)


def stencil(padded, kernel, flip):
    size_x, size_y, depth = (padded.shape[0] - 2, padded.shape[1] - 2, padded.shape[2] - 2)
    taps = kernel.astype(jnp.float32)
    total = jnp.zeros((size_x, size_y, depth, padded.shape[3]), jnp.float32)
    for tap in range(27):
        ox, oy, oz = (tap // 9, tap // 3 % 3, tap % 3)
        if flip:
            ox, oy, oz = (2 - ox, 2 - oy, 2 - oz)
        piece = padded[ox : ox + size_x, oy : oy + size_y, oz : oz + depth]
        total = total + piece.astype(jnp.float32) * taps[tap]
    return total


def inner(field, edge):
    return field[edge : field.shape[0] - edge, edge : field.shape[1] - edge]


def per_device(volume, void_mask, kernel, mix_weight, norm_gain, upstream):
    size_x, size_y, depth, chans = volume.shape
    groups, width = (mix_weight.shape[0], mix_weight.shape[1])
    scale = jnp.float32(size_x * size_y * depth * lax.axis_size("gx") * lax.axis_size("gy"))
    keep_own = (1 - void_mask).astype(jnp.float32)
    rim = 1
    padded_x = halo_2d(volume)
    edge = rim - 1
    padded_z = zwrap(padded_x)
    field = lax.optimization_barrier(stencil(padded_z, kernel, False).astype(jnp.bfloat16)).astype(
        jnp.float32
    )
    ext_x, ext_y = (field.shape[0], field.shape[1])
    field_own = inner(field, edge)
    masked_own = keep_own[..., None] * field_own
    count_part = jnp.sum(keep_own)
    sum_part = jnp.sum(masked_own, axis=(0, 1, 2))
    eye = jnp.eye(width, dtype=jnp.float32)
    mean_part = (sum_part / count_part).reshape(groups, width)
    cent_part = field_own.reshape(size_x, size_y, depth, groups, width) - mean_part
    cov_part = jnp.einsum(
        "abzgi,abzgj->gij", keep_own[..., None, None] * cent_part, cent_part, precision=HI
    )
    moments = butterfly(pack_moments(count_part, mean_part, cov_part), merge_moments)
    count, mean, scatter = unpack_moments(moments)
    count = count[0, 0, 0]
    mean = mean[:, 0]
    sigma = scatter / count + EPS * eye
    white, scaled, ps, as_, bs = whiten_fwd(sigma)
    centered = field.reshape(ext_x, ext_y, depth, groups, width) - mean
    gain = norm_gain.reshape(groups, width)
    pre = jnp.einsum("abzgj,gij->abzgi", centered, white, precision=HI) * gain
    active = jax.nn.silu(pre).astype(jnp.bfloat16)
    active_own = inner(active, edge)
    grad_five = upstream.reshape(ext_x, ext_y, depth, groups, width)
    mixed = jnp.einsum(
        "abzgi,gio->abzgo", active_own, mix_weight, preferred_element_type=jnp.float32
    )
    output = (volume.astype(jnp.float32) + mixed.reshape(size_x, size_y, depth, chans)).astype(
        jnp.bfloat16
    )
    mix_part = jnp.einsum(
        "abzgi,abzgo->gio",
        active_own,
        upstream.reshape(size_x, size_y, depth, groups, width),
        preferred_element_type=jnp.float32,
    )
    (mix_sum,) = butterfly_sum((mix_part,))
    dact = jnp.einsum("abzgo,gio->abzgi", grad_five, mix_weight, preferred_element_type=jnp.float32)
    sig = jax.nn.sigmoid(pre)
    dnormed = dact * sig * (1.0 + pre * (1.0 - sig)) * gain
    dcent = jnp.einsum("abzgi,gij->abzgj", dnormed, white, precision=HI)
    dwhite_part = jnp.einsum(
        "abzgi,abzgj->gij", inner(dnormed, edge), inner(centered, edge), precision=HI
    )
    dsum_part = jnp.sum(inner(dcent, edge), axis=(0, 1, 2))
    dwhite, dsum = butterfly_sum((dwhite_part, dsum_part))
    sens = whiten_bwd(sigma, scaled, ps, as_, bs, dwhite)
    sym = sens + jnp.swapaxes(sens, 1, 2)
    dfield = dcent + keep_own[..., None, None] / count * (
        jnp.einsum("abzgj,gjk->abzgk", centered, sym, precision=HI) - dsum
    )
    dfield = lax.optimization_barrier(
        dfield.astype(jnp.bfloat16).reshape(ext_x, ext_y, depth, chans)
    )
    dfield_pad = zwrap(halo_2d(dfield))
    back = stencil(dfield_pad, kernel, True)
    volume_grad = (upstream.astype(jnp.float32) + back).astype(jnp.bfloat16)
    dfield_own = inner(dfield, edge).astype(jnp.float32)
    ker_terms = []
    for tap in range(27):
        ox, oy, oz = (tap // 9, tap // 3 % 3, tap % 3)
        piece = padded_z[
            edge + ox : edge + ox + size_x, edge + oy : edge + oy + size_y, oz : oz + depth
        ]
        ker_terms.append(jnp.sum(piece.astype(jnp.float32) * dfield_own, axis=(0, 1, 2)))
    ker_part = jnp.stack(ker_terms)
    (ker_sum,) = butterfly_sum((ker_part,))
    return (output, volume_grad, ker_sum / scale, mix_sum / scale)


def solution(mesh):
    in_specs = (
        P("gx", "gy", None, None),
        P("gx", "gy", None),
        P(),
        P(),
        P(),
        P("gx", "gy", None, None),
    )
    out_specs = (P("gx", "gy", None, None), P("gx", "gy", None, None), P(), P())
    return jax.shard_map(
        per_device, mesh=mesh, in_specs=in_specs, out_specs=out_specs, check_vma=False
    )
```

```python
import jax
import jax.numpy as jnp
from jax import lax
from jax.experimental import pallas as pl
from jax.sharding import PartitionSpec as P

SWEEPS = 5


HI = lax.Precision.HIGHEST
EPS = 1e-05


def padded_2(block, sides, width):
    for axis, dim in sides:
        count = lax.axis_size(axis)
        forward = [(i, i + 1) for i in range(count - 1)]
        forward.append((count - 1, 0))
        backward = [(target, source) for source, target in forward]
        low = lax.ppermute(
            lax.slice_in_dim(block, block.shape[dim] - width, None, axis=dim), axis, forward
        )
        high = lax.ppermute(lax.slice_in_dim(block, 0, width, axis=dim), axis, backward)
        block = jnp.concatenate([low, block, high], axis=dim)
    return block


BUTTERFLY = (("gx", 1), ("gx", 2), ("gx", 4), ("gx", 8), ("gx", 16), ("gx", 32), ("gy", 1), ("gy", 2))


def butterfly(value, combine):
    for axis, bit in BUTTERFLY:
        count = lax.axis_size(axis)
        if bit >= count:
            continue
        pairs = [(i, i ^ bit) for i in range(count)]
        value = combine(value, lax.ppermute(value, axis, pairs))
    return value


def butterfly_sum(parts):
    rows = [p.reshape(-1, 128) for p in parts]
    flat = butterfly(jnp.concatenate(rows, axis=0), lambda a, b: a + b)
    out, start = [], 0
    for p, r in zip(parts, rows):
        out.append(flat[start : start + r.shape[0]].reshape(p.shape))
        start += r.shape[0]
    return out


def pack_moments(n, mean, scat):
    groups, width = mean.shape
    count = jnp.broadcast_to(n.reshape(1, 1, 1), (groups, 1, width))
    pad = jnp.zeros((groups, 6, width), jnp.float32)
    return jnp.concatenate([scat, mean[:, None, :], count, pad], axis=1)


def unpack_moments(packed):
    width = packed.shape[2]
    return (packed[:, width + 1 : width + 2], packed[:, width : width + 1], packed[:, :width])


def merge_moments(a, b):
    n_a, mean_a, scat_a = unpack_moments(a)
    n_b, mean_b, scat_b = unpack_moments(b)
    n = n_a + n_b
    mean = (n_a * mean_a + n_b * mean_b) / n
    delta = mean_b - mean_a
    outer = jnp.swapaxes(delta, 1, 2) * delta
    scat = (scat_a + scat_b) + (n_a * n_b / n) * outer
    pad = jnp.zeros_like(a[:, scat.shape[1] + 2 :])
    return jnp.concatenate([scat, mean, n, pad], axis=1)


def whiten(sigma):
    eye = jnp.eye(sigma.shape[0], dtype=sigma.dtype)
    trace = jnp.trace(sigma)
    scaled = sigma / trace
    proj = eye
    for sweep in range(SWEEPS):
        cube = jnp.dot(
            proj, jnp.dot(proj, jnp.dot(proj, scaled, precision=HI), precision=HI), precision=HI
        )
        proj = 1.5 * proj - 0.5 * cube
    return proj / jnp.sqrt(trace)


def mm(a, b):
    return jnp.dot(a, b, precision=HI, preferred_element_type=jnp.float32)


def unit(width):
    rows = lax.broadcasted_iota(jnp.int32, (width, width), 0)
    cols = lax.broadcasted_iota(jnp.int32, (width, width), 1)
    return (rows == cols).astype(jnp.float32)


def whiten_fwd_kernel(sig_ref, white_ref, scaled_ref, ps_ref, as_ref, bs_ref):
    groups, width, _ = sig_ref.shape
    eye = unit(width)
    traces, scaled, proj = [], [], []
    for g in range(groups):
        sig = sig_ref[g]
        trace = jnp.sum(sig * eye, keepdims=True)
        traces.append(trace)
        scaled.append(sig / trace)
        scaled_ref[g] = scaled[g]
        proj.append(eye)
    for sweep in range(SWEEPS):
        first = [mm(proj[g], scaled[g]) for g in range(groups)]
        second = [mm(proj[g], first[g]) for g in range(groups)]
        cube = [mm(proj[g], second[g]) for g in range(groups)]
        for g in range(groups):
            ps_ref[g, sweep] = proj[g]
            as_ref[g, sweep] = first[g]
            bs_ref[g, sweep] = second[g]
            proj[g] = 1.5 * proj[g] - 0.5 * cube[g]
    for g in range(groups):
        ps_ref[g, SWEEPS] = proj[g]
        white_ref[g] = proj[g] / jnp.sqrt(traces[g])


def whiten_bwd_kernel(sig_ref, scaled_ref, ps_ref, as_ref, bs_ref, dwhite_ref, sens_ref):
    groups, width, _ = sig_ref.shape
    eye = unit(width)
    traces, roots, grad, grad_trace, grad_scaled = [], [], [], [], []
    for g in range(groups):
        sig = sig_ref[g]
        trace = jnp.sum(sig * eye, keepdims=True)
        root = jnp.sqrt(trace)
        dwhite = dwhite_ref[g]
        traces.append(trace)
        grad.append(dwhite / root)
        grad_trace.append(-0.5 * jnp.sum(dwhite * ps_ref[g, SWEEPS], keepdims=True) / (trace * root))
        grad_scaled.append(jnp.zeros_like(sig))
    for sweep in reversed(range(SWEEPS)):
        proj = [ps_ref[g, sweep] for g in range(groups)]
        grad_cube = [-0.5 * grad[g] for g in range(groups)]
        grad_second = [mm(proj[g], grad_cube[g]) for g in range(groups)]
        grad_first = [mm(proj[g], grad_second[g]) for g in range(groups)]
        for g in range(groups):
            grad_scaled[g] = grad_scaled[g] + mm(proj[g], grad_first[g])
            grad[g] = (
                1.5 * grad[g]
                + mm(grad_cube[g], bs_ref[g, sweep])
                + mm(grad_second[g], as_ref[g, sweep])
                + mm(grad_first[g], scaled_ref[g])
            )
    for g in range(groups):
        trace = traces[g]
        total = grad_trace[g] - jnp.sum(grad_scaled[g] * sig_ref[g], keepdims=True) / (trace * trace)
        sens_ref[g] = grad_scaled[g] / trace + total * eye


def whiten_fwd(sigma):
    groups, width, _ = sigma.shape
    f32 = jnp.float32
    return pl.pallas_call(
        whiten_fwd_kernel,
        out_shape=[
            jax.ShapeDtypeStruct((groups, width, width), f32),
            jax.ShapeDtypeStruct((groups, width, width), f32),
            jax.ShapeDtypeStruct((groups, SWEEPS + 1, width, width), f32),
            jax.ShapeDtypeStruct((groups, SWEEPS, width, width), f32),
            jax.ShapeDtypeStruct((groups, SWEEPS, width, width), f32),
        ],
    )(sigma)


def whiten_bwd(sigma, scaled, ps, as_, bs, dwhite):
    groups, width, _ = sigma.shape
    return pl.pallas_call(
        whiten_bwd_kernel,
        out_shape=jax.ShapeDtypeStruct((groups, width, width), jnp.float32),
    )(sigma, scaled, ps, as_, bs, dwhite)


def zwrap(field):
    return jnp.concatenate([field[:, :, -1:], field, field[:, :, :1]], axis=2)


def stencil(padded, kernel, flip):
    size_x, size_y, depth = (padded.shape[0] - 2, padded.shape[1] - 2, padded.shape[2] - 2)
    taps = kernel.astype(jnp.float32)
    total = jnp.zeros((size_x, size_y, depth, padded.shape[3]), jnp.float32)
    for tap in range(27):
        ox, oy, oz = (tap // 9, tap // 3 % 3, tap % 3)
        if flip:
            ox, oy, oz = (2 - ox, 2 - oy, 2 - oz)
        piece = padded[ox : ox + size_x, oy : oy + size_y, oz : oz + depth]
        total = total + piece.astype(jnp.float32) * taps[tap]
    return total


def inner(field, edge):
    return field[edge : field.shape[0] - edge, edge : field.shape[1] - edge]


def per_device(volume, void_mask, kernel, mix_weight, norm_gain, upstream):
    size_x, size_y, depth, chans = volume.shape
    groups, width = (mix_weight.shape[0], mix_weight.shape[1])
    scale = jnp.float32(size_x * size_y * depth * lax.axis_size("gx") * lax.axis_size("gy"))
    keep_own = (1 - void_mask).astype(jnp.float32)
    rim = 1
    padded_x = padded_2(volume, (("gx", 0), ("gy", 1)), 1)
    edge = rim - 1
    padded_z = zwrap(padded_x)
    field = lax.optimization_barrier(stencil(padded_z, kernel, False).astype(jnp.bfloat16)).astype(
        jnp.float32
    )
    ext_x, ext_y = (field.shape[0], field.shape[1])
    field_own = inner(field, edge)
    masked_own = keep_own[..., None] * field_own
    count_part = jnp.sum(keep_own)
    sum_part = jnp.sum(masked_own, axis=(0, 1, 2))
    eye = jnp.eye(width, dtype=jnp.float32)
    mean_part = (sum_part / count_part).reshape(groups, width)
    cent_part = field_own.reshape(size_x, size_y, depth, groups, width) - mean_part
    cov_part = jnp.einsum(
        "abzgi,abzgj->gij", keep_own[..., None, None] * cent_part, cent_part, precision=HI
    )
    moments = butterfly(pack_moments(count_part, mean_part, cov_part), merge_moments)
    count, mean, scatter = unpack_moments(moments)
    count = count[0, 0, 0]
    mean = mean[:, 0]
    sigma = scatter / count + EPS * eye
    white, scaled, ps, as_, bs = whiten_fwd(sigma)
    centered = field.reshape(ext_x, ext_y, depth, groups, width) - mean
    gain = norm_gain.reshape(groups, width)
    pre = jnp.einsum("abzgj,gij->abzgi", centered, white, precision=HI) * gain
    active = jax.nn.silu(pre).astype(jnp.bfloat16)
    active_own = inner(active, edge)
    grad_five = upstream.reshape(ext_x, ext_y, depth, groups, width)
    mixed = jnp.einsum(
        "abzgi,gio->abzgo", active_own, mix_weight, preferred_element_type=jnp.float32
    )
    output = (volume.astype(jnp.float32) + mixed.reshape(size_x, size_y, depth, chans)).astype(
        jnp.bfloat16
    )
    mix_part = jnp.einsum(
        "abzgi,abzgo->gio",
        active_own,
        upstream.reshape(size_x, size_y, depth, groups, width),
        preferred_element_type=jnp.float32,
    )
    dact = jnp.einsum("abzgo,gio->abzgi", grad_five, mix_weight, preferred_element_type=jnp.float32)
    sig = jax.nn.sigmoid(pre)
    dnormed = dact * sig * (1.0 + pre * (1.0 - sig)) * gain
    dcent = jnp.einsum("abzgi,gij->abzgj", dnormed, white, precision=HI)
    dwhite_part = jnp.einsum(
        "abzgi,abzgj->gij", inner(dnormed, edge), inner(centered, edge), precision=HI
    )
    dsum_part = jnp.sum(inner(dcent, edge), axis=(0, 1, 2))
    dwhite, dsum = butterfly_sum((dwhite_part, dsum_part))
    sens = whiten_bwd(sigma, scaled, ps, as_, bs, dwhite)
    sym = sens + jnp.swapaxes(sens, 1, 2)
    dfield = dcent + keep_own[..., None, None] / count * (
        jnp.einsum("abzgj,gjk->abzgk", centered, sym, precision=HI) - dsum
    )
    dfield = lax.optimization_barrier(
        dfield.astype(jnp.bfloat16).reshape(ext_x, ext_y, depth, chans)
    )
    dfield_pad = zwrap(padded_2(dfield, (("gx", 0), ("gy", 1)), 1))
    back = stencil(dfield_pad, kernel, True)
    volume_grad = (upstream.astype(jnp.float32) + back).astype(jnp.bfloat16)
    dfield_own = inner(dfield, edge).astype(jnp.float32)
    ker_terms = []
    for tap in range(27):
        ox, oy, oz = (tap // 9, tap // 3 % 3, tap % 3)
        piece = padded_z[
            edge + ox : edge + ox + size_x, edge + oy : edge + oy + size_y, oz : oz + depth
        ]
        ker_terms.append(jnp.sum(piece.astype(jnp.float32) * dfield_own, axis=(0, 1, 2)))
    ker_part = jnp.stack(ker_terms)
    ker_sum, mix_sum = butterfly_sum((ker_part, mix_part))
    return (output, volume_grad, ker_sum / scale, mix_sum / scale)


def solution(mesh):
    in_specs = (
        P("gx", "gy", None, None),
        P("gx", "gy", None),
        P(),
        P(),
        P(),
        P("gx", "gy", None, None),
    )
    out_specs = (P("gx", "gy", None, None), P("gx", "gy", None, None), P(), P())
    return jax.shard_map(
        per_device, mesh=mesh, in_specs=in_specs, out_specs=out_specs, check_vma=False
    )
```

```python
import jax
import jax.numpy as jnp
from jax import lax
from jax.experimental import pallas as pl
from jax.sharding import PartitionSpec as P

SWEEPS = 5


HI = lax.Precision.HIGHEST
EPS = 1e-05


def padded_2(block, sides, width):
    for axis, dim in sides:
        count = lax.axis_size(axis)
        forward = [(i, i + 1) for i in range(count - 1)]
        forward.append((count - 1, 0))
        backward = [(target, source) for source, target in forward]
        low = lax.ppermute(
            lax.slice_in_dim(block, block.shape[dim] - width, None, axis=dim), axis, forward
        )
        high = lax.ppermute(lax.slice_in_dim(block, 0, width, axis=dim), axis, backward)
        block = jnp.concatenate([low, block, high], axis=dim)
    return block


BUTTERFLY = (("gx", 1), ("gx", 2), ("gx", 4), ("gx", 8), ("gx", 16), ("gx", 32), ("gy", 1), ("gy", 2))


def butterfly(value, combine):
    for axis, bit in BUTTERFLY:
        count = lax.axis_size(axis)
        if bit >= count:
            continue
        pairs = [(i, i ^ bit) for i in range(count)]
        value = combine(value, lax.ppermute(value, axis, pairs))
    return value


def exchange_sum(parts):
    axes = ("gx", "gy")
    devices = lax.axis_size(axes)
    rows = [p.reshape(-1, 128) for p in parts]
    flat = jnp.concatenate(rows, axis=0)
    total = flat.shape[0]
    per = -(-total // devices)
    flat = jnp.pad(flat, ((0, per * devices - total), (0, 0))).reshape(devices, per, 128)
    got = lax.all_to_all(flat, axes, 0, 0, tiled=True)
    mine = jnp.sum(got, axis=0, keepdims=True)
    back = lax.all_to_all(jnp.broadcast_to(mine, flat.shape), axes, 0, 0, tiled=True)
    back = back.reshape(per * devices, 128)
    out, start = [], 0
    for p, r in zip(parts, rows):
        out.append(back[start : start + r.shape[0]].reshape(p.shape))
        start += r.shape[0]
    return out


def pack_moments(n, mean, scat):
    groups, width = mean.shape
    count = jnp.broadcast_to(n.reshape(1, 1, 1), (groups, 1, width))
    pad = jnp.zeros((groups, 6, width), jnp.float32)
    return jnp.concatenate([scat, mean[:, None, :], count, pad], axis=1)


def unpack_moments(packed):
    width = packed.shape[2]
    return (packed[:, width + 1 : width + 2], packed[:, width : width + 1], packed[:, :width])


def merge_moments(a, b):
    n_a, mean_a, scat_a = unpack_moments(a)
    n_b, mean_b, scat_b = unpack_moments(b)
    n = n_a + n_b
    mean = (n_a * mean_a + n_b * mean_b) / n
    delta = mean_b - mean_a
    outer = jnp.swapaxes(delta, 1, 2) * delta
    scat = (scat_a + scat_b) + (n_a * n_b / n) * outer
    pad = jnp.zeros_like(a[:, scat.shape[1] + 2 :])
    return jnp.concatenate([scat, mean, n, pad], axis=1)


def whiten(sigma):
    eye = jnp.eye(sigma.shape[0], dtype=sigma.dtype)
    trace = jnp.trace(sigma)
    scaled = sigma / trace
    proj = eye
    for sweep in range(SWEEPS):
        cube = jnp.dot(
            proj, jnp.dot(proj, jnp.dot(proj, scaled, precision=HI), precision=HI), precision=HI
        )
        proj = 1.5 * proj - 0.5 * cube
    return proj / jnp.sqrt(trace)


def mm(a, b):
    return jnp.dot(a, b, precision=HI, preferred_element_type=jnp.float32)


def unit(width):
    rows = lax.broadcasted_iota(jnp.int32, (width, width), 0)
    cols = lax.broadcasted_iota(jnp.int32, (width, width), 1)
    return (rows == cols).astype(jnp.float32)


def whiten_fwd_kernel(sig_ref, white_ref, scaled_ref, ps_ref, as_ref, bs_ref):
    groups, width, _ = sig_ref.shape
    eye = unit(width)
    traces, scaled, proj = [], [], []
    for g in range(groups):
        sig = sig_ref[g]
        trace = jnp.sum(sig * eye, keepdims=True)
        traces.append(trace)
        scaled.append(sig / trace)
        scaled_ref[g] = scaled[g]
        proj.append(eye)
    for sweep in range(SWEEPS):
        first = [mm(proj[g], scaled[g]) for g in range(groups)]
        second = [mm(proj[g], first[g]) for g in range(groups)]
        cube = [mm(proj[g], second[g]) for g in range(groups)]
        for g in range(groups):
            ps_ref[g, sweep] = proj[g]
            as_ref[g, sweep] = first[g]
            bs_ref[g, sweep] = second[g]
            proj[g] = 1.5 * proj[g] - 0.5 * cube[g]
    for g in range(groups):
        ps_ref[g, SWEEPS] = proj[g]
        white_ref[g] = proj[g] / jnp.sqrt(traces[g])


def whiten_bwd_kernel(sig_ref, scaled_ref, ps_ref, as_ref, bs_ref, dwhite_ref, sens_ref):
    groups, width, _ = sig_ref.shape
    eye = unit(width)
    traces, roots, grad, grad_trace, grad_scaled = [], [], [], [], []
    for g in range(groups):
        sig = sig_ref[g]
        trace = jnp.sum(sig * eye, keepdims=True)
        root = jnp.sqrt(trace)
        dwhite = dwhite_ref[g]
        traces.append(trace)
        grad.append(dwhite / root)
        grad_trace.append(-0.5 * jnp.sum(dwhite * ps_ref[g, SWEEPS], keepdims=True) / (trace * root))
        grad_scaled.append(jnp.zeros_like(sig))
    for sweep in reversed(range(SWEEPS)):
        proj = [ps_ref[g, sweep] for g in range(groups)]
        grad_cube = [-0.5 * grad[g] for g in range(groups)]
        grad_second = [mm(proj[g], grad_cube[g]) for g in range(groups)]
        grad_first = [mm(proj[g], grad_second[g]) for g in range(groups)]
        for g in range(groups):
            grad_scaled[g] = grad_scaled[g] + mm(proj[g], grad_first[g])
            grad[g] = (
                1.5 * grad[g]
                + mm(grad_cube[g], bs_ref[g, sweep])
                + mm(grad_second[g], as_ref[g, sweep])
                + mm(grad_first[g], scaled_ref[g])
            )
    for g in range(groups):
        trace = traces[g]
        total = grad_trace[g] - jnp.sum(grad_scaled[g] * sig_ref[g], keepdims=True) / (trace * trace)
        sens_ref[g] = grad_scaled[g] / trace + total * eye


def whiten_fwd(sigma):
    groups, width, _ = sigma.shape
    f32 = jnp.float32
    return pl.pallas_call(
        whiten_fwd_kernel,
        out_shape=[
            jax.ShapeDtypeStruct((groups, width, width), f32),
            jax.ShapeDtypeStruct((groups, width, width), f32),
            jax.ShapeDtypeStruct((groups, SWEEPS + 1, width, width), f32),
            jax.ShapeDtypeStruct((groups, SWEEPS, width, width), f32),
            jax.ShapeDtypeStruct((groups, SWEEPS, width, width), f32),
        ],
    )(sigma)


def whiten_bwd(sigma, scaled, ps, as_, bs, dwhite):
    groups, width, _ = sigma.shape
    return pl.pallas_call(
        whiten_bwd_kernel,
        out_shape=jax.ShapeDtypeStruct((groups, width, width), jnp.float32),
    )(sigma, scaled, ps, as_, bs, dwhite)


def zwrap(field):
    return jnp.concatenate([field[:, :, -1:], field, field[:, :, :1]], axis=2)


def stencil(padded, kernel, flip):
    size_x, size_y, depth = (padded.shape[0] - 2, padded.shape[1] - 2, padded.shape[2] - 2)
    taps = kernel.astype(jnp.float32)
    total = jnp.zeros((size_x, size_y, depth, padded.shape[3]), jnp.float32)
    for tap in range(27):
        ox, oy, oz = (tap // 9, tap // 3 % 3, tap % 3)
        if flip:
            ox, oy, oz = (2 - ox, 2 - oy, 2 - oz)
        piece = padded[ox : ox + size_x, oy : oy + size_y, oz : oz + depth]
        total = total + piece.astype(jnp.float32) * taps[tap]
    return total


def inner(field, edge):
    return field[edge : field.shape[0] - edge, edge : field.shape[1] - edge]


def per_device(volume, void_mask, kernel, mix_weight, norm_gain, upstream):
    size_x, size_y, depth, chans = volume.shape
    groups, width = (mix_weight.shape[0], mix_weight.shape[1])
    scale = jnp.float32(size_x * size_y * depth * lax.axis_size("gx") * lax.axis_size("gy"))
    keep_own = (1 - void_mask).astype(jnp.float32)
    rim = 1
    padded_x = padded_2(volume, (("gx", 0), ("gy", 1)), 1)
    edge = rim - 1
    padded_z = zwrap(padded_x)
    field = lax.optimization_barrier(stencil(padded_z, kernel, False).astype(jnp.bfloat16)).astype(
        jnp.float32
    )
    ext_x, ext_y = (field.shape[0], field.shape[1])
    field_own = inner(field, edge)
    masked_own = keep_own[..., None] * field_own
    count_part = jnp.sum(keep_own)
    sum_part = jnp.sum(masked_own, axis=(0, 1, 2))
    eye = jnp.eye(width, dtype=jnp.float32)
    mean_part = (sum_part / count_part).reshape(groups, width)
    cent_part = field_own.reshape(size_x, size_y, depth, groups, width) - mean_part
    cov_part = jnp.einsum(
        "abzgi,abzgj->gij", keep_own[..., None, None] * cent_part, cent_part, precision=HI
    )
    moments = butterfly(pack_moments(count_part, mean_part, cov_part), merge_moments)
    count, mean, scatter = unpack_moments(moments)
    count = count[0, 0, 0]
    mean = mean[:, 0]
    sigma = scatter / count + EPS * eye
    white, scaled, ps, as_, bs = whiten_fwd(sigma)
    centered = field.reshape(ext_x, ext_y, depth, groups, width) - mean
    gain = norm_gain.reshape(groups, width)
    pre = jnp.einsum("abzgj,gij->abzgi", centered, white, precision=HI) * gain
    active = jax.nn.silu(pre).astype(jnp.bfloat16)
    active_own = inner(active, edge)
    grad_five = upstream.reshape(ext_x, ext_y, depth, groups, width)
    mixed = jnp.einsum(
        "abzgi,gio->abzgo", active_own, mix_weight, preferred_element_type=jnp.float32
    )
    output = (volume.astype(jnp.float32) + mixed.reshape(size_x, size_y, depth, chans)).astype(
        jnp.bfloat16
    )
    mix_part = jnp.einsum(
        "abzgi,abzgo->gio",
        active_own,
        upstream.reshape(size_x, size_y, depth, groups, width),
        preferred_element_type=jnp.float32,
    )
    dact = jnp.einsum("abzgo,gio->abzgi", grad_five, mix_weight, preferred_element_type=jnp.float32)
    sig = jax.nn.sigmoid(pre)
    dnormed = dact * sig * (1.0 + pre * (1.0 - sig)) * gain
    dcent = jnp.einsum("abzgi,gij->abzgj", dnormed, white, precision=HI)
    dwhite_part = jnp.einsum(
        "abzgi,abzgj->gij", inner(dnormed, edge), inner(centered, edge), precision=HI
    )
    dsum_part = jnp.sum(inner(dcent, edge), axis=(0, 1, 2))
    dwhite, dsum = exchange_sum((dwhite_part, dsum_part))
    sens = whiten_bwd(sigma, scaled, ps, as_, bs, dwhite)
    sym = sens + jnp.swapaxes(sens, 1, 2)
    dfield = dcent + keep_own[..., None, None] / count * (
        jnp.einsum("abzgj,gjk->abzgk", centered, sym, precision=HI) - dsum
    )
    dfield = lax.optimization_barrier(
        dfield.astype(jnp.bfloat16).reshape(ext_x, ext_y, depth, chans)
    )
    dfield_pad = zwrap(padded_2(dfield, (("gx", 0), ("gy", 1)), 1))
    back = stencil(dfield_pad, kernel, True)
    volume_grad = (upstream.astype(jnp.float32) + back).astype(jnp.bfloat16)
    dfield_own = inner(dfield, edge).astype(jnp.float32)
    ker_terms = []
    for tap in range(27):
        ox, oy, oz = (tap // 9, tap // 3 % 3, tap % 3)
        piece = padded_z[
            edge + ox : edge + ox + size_x, edge + oy : edge + oy + size_y, oz : oz + depth
        ]
        ker_terms.append(jnp.sum(piece.astype(jnp.float32) * dfield_own, axis=(0, 1, 2)))
    ker_part = jnp.stack(ker_terms)
    ker_sum, mix_sum = exchange_sum((ker_part, mix_part))
    return (output, volume_grad, ker_sum / scale, mix_sum / scale)


def solution(mesh):
    in_specs = (
        P("gx", "gy", None, None),
        P("gx", "gy", None),
        P(),
        P(),
        P(),
        P("gx", "gy", None, None),
    )
    out_specs = (P("gx", "gy", None, None), P("gx", "gy", None, None), P(), P())
    return jax.shard_map(
        per_device, mesh=mesh, in_specs=in_specs, out_specs=out_specs, check_vma=False
    )
```

```python
import jax
import jax.numpy as jnp
from jax import lax
from jax.experimental import pallas as pl
from jax.sharding import PartitionSpec as P

SWEEPS = 5


HI = lax.Precision.HIGHEST
EPS = 1e-05


def padded_2(block, sides, width):
    for axis, dim in sides:
        count = lax.axis_size(axis)
        forward = [(i, i + 1) for i in range(count - 1)]
        forward.append((count - 1, 0))
        backward = [(target, source) for source, target in forward]
        low = lax.ppermute(
            lax.slice_in_dim(block, block.shape[dim] - width, None, axis=dim), axis, forward
        )
        high = lax.ppermute(lax.slice_in_dim(block, 0, width, axis=dim), axis, backward)
        block = jnp.concatenate([low, block, high], axis=dim)
    return block


BUTTERFLY = (("gx", 1), ("gx", 2), ("gx", 4), ("gx", 8), ("gx", 16), ("gx", 32), ("gy", 1), ("gy", 2))


def butterfly(value, combine):
    for axis, bit in BUTTERFLY:
        count = lax.axis_size(axis)
        if bit >= count:
            continue
        pairs = [(i, i ^ bit) for i in range(count)]
        value = combine(value, lax.ppermute(value, axis, pairs))
    return value


def butterfly_sum(parts):
    rows = [p.reshape(-1, 128) for p in parts]
    flat = butterfly(jnp.concatenate(rows, axis=0), lambda a, b: a + b)
    out, start = [], 0
    for p, r in zip(parts, rows):
        out.append(flat[start : start + r.shape[0]].reshape(p.shape))
        start += r.shape[0]
    return out


def tri_masks(width):
    rows = lax.broadcasted_iota(jnp.int32, (width, width), 0)
    cols = lax.broadcasted_iota(jnp.int32, (width, width), 1)
    return (cols >= rows, rows > cols)


def pack_moments(n, mean, scat):
    groups, width = mean.shape
    upper, _ = tri_masks(width)
    eye = jnp.eye(width, dtype=jnp.float32)
    block = jnp.where(upper, scat[0::2], scat[1::2])
    diag_odd = jnp.sum(scat[1::2] * eye, axis=1, keepdims=True)
    count = jnp.broadcast_to(n.reshape(1, 1, 1), (groups // 2, 1, width))
    pad = jnp.zeros((groups // 2, 4, width), jnp.float32)
    parts = [block, diag_odd, mean[0::2, None, :], mean[1::2, None, :], count, pad]
    return jnp.concatenate(parts, axis=1)


def merge_moments(a, b):
    width = a.shape[2]
    upper, _ = tri_masks(width)
    n_a, n_b = (a[:, width + 3 : width + 4], b[:, width + 3 : width + 4])
    n = n_a + n_b
    weight = n_a * n_b / n
    even_a, even_b = (a[:, width + 1 : width + 2], b[:, width + 1 : width + 2])
    odd_a, odd_b = (a[:, width + 2 : width + 3], b[:, width + 2 : width + 3])
    even = (n_a * even_a + n_b * even_b) / n
    odd = (n_a * odd_a + n_b * odd_b) / n
    d_even = even_b - even_a
    d_odd = odd_b - odd_a
    outer = jnp.where(
        upper, jnp.swapaxes(d_even, 1, 2) * d_even, jnp.swapaxes(d_odd, 1, 2) * d_odd
    )
    block = (a[:, :width] + b[:, :width]) + weight * outer
    diag = (a[:, width : width + 1] + b[:, width : width + 1]) + weight * (d_odd * d_odd)
    pad = jnp.zeros_like(a[:, width + 4 :])
    return jnp.concatenate([block, diag, even, odd, n, pad], axis=1)


def unpack_moments(packed):
    pairs, _, width = packed.shape
    upper, lower = tri_masks(width)
    block = packed[:, :width]
    flipped = jnp.swapaxes(block, 1, 2)
    even = jnp.where(upper, block, flipped)
    diag = jnp.broadcast_to(packed[:, width : width + 1], block.shape)
    strict_upper = jnp.swapaxes(lower, 0, 1)
    odd = jnp.where(lower, block, jnp.where(strict_upper, flipped, diag))
    scat = jnp.stack([even, odd], axis=1).reshape(2 * pairs, width, width)
    mean = jnp.concatenate([packed[:, width + 1 : width + 2], packed[:, width + 2 : width + 3]], axis=1)
    return (packed[0, width + 3, 0], mean.reshape(2 * pairs, width), scat)


def whiten(sigma):
    eye = jnp.eye(sigma.shape[0], dtype=sigma.dtype)
    trace = jnp.trace(sigma)
    scaled = sigma / trace
    proj = eye
    for sweep in range(SWEEPS):
        cube = jnp.dot(
            proj, jnp.dot(proj, jnp.dot(proj, scaled, precision=HI), precision=HI), precision=HI
        )
        proj = 1.5 * proj - 0.5 * cube
    return proj / jnp.sqrt(trace)


def mm(a, b):
    return jnp.dot(a, b, precision=HI, preferred_element_type=jnp.float32)


def unit(width):
    rows = lax.broadcasted_iota(jnp.int32, (width, width), 0)
    cols = lax.broadcasted_iota(jnp.int32, (width, width), 1)
    return (rows == cols).astype(jnp.float32)


def whiten_fwd_kernel(sig_ref, white_ref, scaled_ref, ps_ref, as_ref, bs_ref):
    groups, width, _ = sig_ref.shape
    eye = unit(width)
    traces, scaled, proj = [], [], []
    for g in range(groups):
        sig = sig_ref[g]
        trace = jnp.sum(sig * eye, keepdims=True)
        traces.append(trace)
        scaled.append(sig / trace)
        scaled_ref[g] = scaled[g]
        proj.append(eye)
    for sweep in range(SWEEPS):
        first = [mm(proj[g], scaled[g]) for g in range(groups)]
        second = [mm(proj[g], first[g]) for g in range(groups)]
        cube = [mm(proj[g], second[g]) for g in range(groups)]
        for g in range(groups):
            ps_ref[g, sweep] = proj[g]
            as_ref[g, sweep] = first[g]
            bs_ref[g, sweep] = second[g]
            proj[g] = 1.5 * proj[g] - 0.5 * cube[g]
    for g in range(groups):
        ps_ref[g, SWEEPS] = proj[g]
        white_ref[g] = proj[g] / jnp.sqrt(traces[g])


def whiten_bwd_kernel(sig_ref, scaled_ref, ps_ref, as_ref, bs_ref, dwhite_ref, sens_ref):
    groups, width, _ = sig_ref.shape
    eye = unit(width)
    traces, roots, grad, grad_trace, grad_scaled = [], [], [], [], []
    for g in range(groups):
        sig = sig_ref[g]
        trace = jnp.sum(sig * eye, keepdims=True)
        root = jnp.sqrt(trace)
        dwhite = dwhite_ref[g]
        traces.append(trace)
        grad.append(dwhite / root)
        grad_trace.append(-0.5 * jnp.sum(dwhite * ps_ref[g, SWEEPS], keepdims=True) / (trace * root))
        grad_scaled.append(jnp.zeros_like(sig))
    for sweep in reversed(range(SWEEPS)):
        proj = [ps_ref[g, sweep] for g in range(groups)]
        grad_cube = [-0.5 * grad[g] for g in range(groups)]
        grad_second = [mm(proj[g], grad_cube[g]) for g in range(groups)]
        grad_first = [mm(proj[g], grad_second[g]) for g in range(groups)]
        for g in range(groups):
            grad_scaled[g] = grad_scaled[g] + mm(proj[g], grad_first[g])
            grad[g] = (
                1.5 * grad[g]
                + mm(grad_cube[g], bs_ref[g, sweep])
                + mm(grad_second[g], as_ref[g, sweep])
                + mm(grad_first[g], scaled_ref[g])
            )
    for g in range(groups):
        trace = traces[g]
        total = grad_trace[g] - jnp.sum(grad_scaled[g] * sig_ref[g], keepdims=True) / (trace * trace)
        sens_ref[g] = grad_scaled[g] / trace + total * eye


def whiten_fwd(sigma):
    groups, width, _ = sigma.shape
    f32 = jnp.float32
    return pl.pallas_call(
        whiten_fwd_kernel,
        out_shape=[
            jax.ShapeDtypeStruct((groups, width, width), f32),
            jax.ShapeDtypeStruct((groups, width, width), f32),
            jax.ShapeDtypeStruct((groups, SWEEPS + 1, width, width), f32),
            jax.ShapeDtypeStruct((groups, SWEEPS, width, width), f32),
            jax.ShapeDtypeStruct((groups, SWEEPS, width, width), f32),
        ],
    )(sigma)


def whiten_bwd(sigma, scaled, ps, as_, bs, dwhite):
    groups, width, _ = sigma.shape
    return pl.pallas_call(
        whiten_bwd_kernel,
        out_shape=jax.ShapeDtypeStruct((groups, width, width), jnp.float32),
    )(sigma, scaled, ps, as_, bs, dwhite)


def zwrap(field):
    return jnp.concatenate([field[:, :, -1:], field, field[:, :, :1]], axis=2)


def stencil(padded, kernel, flip):
    size_x, size_y, depth = (padded.shape[0] - 2, padded.shape[1] - 2, padded.shape[2] - 2)
    taps = kernel.astype(jnp.float32)
    total = jnp.zeros((size_x, size_y, depth, padded.shape[3]), jnp.float32)
    for tap in range(27):
        ox, oy, oz = (tap // 9, tap // 3 % 3, tap % 3)
        if flip:
            ox, oy, oz = (2 - ox, 2 - oy, 2 - oz)
        piece = padded[ox : ox + size_x, oy : oy + size_y, oz : oz + depth]
        total = total + piece.astype(jnp.float32) * taps[tap]
    return total


def inner(field, edge):
    return field[edge : field.shape[0] - edge, edge : field.shape[1] - edge]


def per_device(volume, void_mask, kernel, mix_weight, norm_gain, upstream):
    size_x, size_y, depth, chans = volume.shape
    groups, width = (mix_weight.shape[0], mix_weight.shape[1])
    scale = jnp.float32(size_x * size_y * depth * lax.axis_size("gx") * lax.axis_size("gy"))
    keep_own = (1 - void_mask).astype(jnp.float32)
    rim = 1
    padded_x = padded_2(volume, (("gx", 0), ("gy", 1)), 1)
    edge = rim - 1
    padded_z = zwrap(padded_x)
    field = lax.optimization_barrier(stencil(padded_z, kernel, False).astype(jnp.bfloat16)).astype(
        jnp.float32
    )
    ext_x, ext_y = (field.shape[0], field.shape[1])
    field_own = inner(field, edge)
    masked_own = keep_own[..., None] * field_own
    count_part = jnp.sum(keep_own)
    sum_part = jnp.sum(masked_own, axis=(0, 1, 2))
    eye = jnp.eye(width, dtype=jnp.float32)
    mean_part = (sum_part / count_part).reshape(groups, width)
    cent_part = field_own.reshape(size_x, size_y, depth, groups, width) - mean_part
    cov_part = jnp.einsum(
        "abzgi,abzgj->gij", keep_own[..., None, None] * cent_part, cent_part, precision=HI
    )
    moments = butterfly(pack_moments(count_part, mean_part, cov_part), merge_moments)
    count, mean, scatter = unpack_moments(moments)
    sigma = scatter / count + EPS * eye
    white, scaled, ps, as_, bs = whiten_fwd(sigma)
    centered = field.reshape(ext_x, ext_y, depth, groups, width) - mean
    gain = norm_gain.reshape(groups, width)
    pre = jnp.einsum("abzgj,gij->abzgi", centered, white, precision=HI) * gain
    active = jax.nn.silu(pre).astype(jnp.bfloat16)
    active_own = inner(active, edge)
    grad_five = upstream.reshape(ext_x, ext_y, depth, groups, width)
    mixed = jnp.einsum(
        "abzgi,gio->abzgo", active_own, mix_weight, preferred_element_type=jnp.float32
    )
    output = (volume.astype(jnp.float32) + mixed.reshape(size_x, size_y, depth, chans)).astype(
        jnp.bfloat16
    )
    mix_part = jnp.einsum(
        "abzgi,abzgo->gio",
        active_own,
        upstream.reshape(size_x, size_y, depth, groups, width),
        preferred_element_type=jnp.float32,
    )
    dact = jnp.einsum("abzgo,gio->abzgi", grad_five, mix_weight, preferred_element_type=jnp.float32)
    sig = jax.nn.sigmoid(pre)
    dnormed = dact * sig * (1.0 + pre * (1.0 - sig)) * gain
    dcent = jnp.einsum("abzgi,gij->abzgj", dnormed, white, precision=HI)
    dwhite_part = jnp.einsum(
        "abzgi,abzgj->gij", inner(dnormed, edge), inner(centered, edge), precision=HI
    )
    dsum_part = jnp.sum(inner(dcent, edge), axis=(0, 1, 2))
    dwhite, dsum = butterfly_sum((dwhite_part, dsum_part))
    sens = whiten_bwd(sigma, scaled, ps, as_, bs, dwhite)
    sym = sens + jnp.swapaxes(sens, 1, 2)
    dfield = dcent + keep_own[..., None, None] / count * (
        jnp.einsum("abzgj,gjk->abzgk", centered, sym, precision=HI) - dsum
    )
    dfield = lax.optimization_barrier(
        dfield.astype(jnp.bfloat16).reshape(ext_x, ext_y, depth, chans)
    )
    dfield_pad = zwrap(padded_2(dfield, (("gx", 0), ("gy", 1)), 1))
    back = stencil(dfield_pad, kernel, True)
    volume_grad = (upstream.astype(jnp.float32) + back).astype(jnp.bfloat16)
    dfield_own = inner(dfield, edge).astype(jnp.float32)
    ker_terms = []
    for tap in range(27):
        ox, oy, oz = (tap // 9, tap // 3 % 3, tap % 3)
        piece = padded_z[
            edge + ox : edge + ox + size_x, edge + oy : edge + oy + size_y, oz : oz + depth
        ]
        ker_terms.append(jnp.sum(piece.astype(jnp.float32) * dfield_own, axis=(0, 1, 2)))
    ker_part = jnp.stack(ker_terms)
    ker_sum, mix_sum = butterfly_sum((ker_part, mix_part))
    return (output, volume_grad, ker_sum / scale, mix_sum / scale)


def solution(mesh):
    in_specs = (
        P("gx", "gy", None, None),
        P("gx", "gy", None),
        P(),
        P(),
        P(),
        P("gx", "gy", None, None),
    )
    out_specs = (P("gx", "gy", None, None), P("gx", "gy", None, None), P(), P())
    return jax.shard_map(
        per_device, mesh=mesh, in_specs=in_specs, out_specs=out_specs, check_vma=False
    )
```

```python
import jax
import jax.numpy as jnp
from jax import lax
from jax.experimental import pallas as pl
from jax.sharding import PartitionSpec as P

SWEEPS = 5


HI = lax.Precision.HIGHEST
EPS = 1e-05


def padded_2(block, sides, width):
    for axis, dim in sides:
        count = lax.axis_size(axis)
        forward = [(i, i + 1) for i in range(count - 1)]
        forward.append((count - 1, 0))
        backward = [(target, source) for source, target in forward]
        low = lax.ppermute(
            lax.slice_in_dim(block, block.shape[dim] - width, None, axis=dim), axis, forward
        )
        high = lax.ppermute(lax.slice_in_dim(block, 0, width, axis=dim), axis, backward)
        block = jnp.concatenate([low, block, high], axis=dim)
    return block


BUTTERFLY = (("gx", 1), ("gx", 2), ("gx", 4), ("gx", 8), ("gx", 16), ("gx", 32), ("gy", 1), ("gy", 2))


def butterfly(value, combine):
    for axis, bit in BUTTERFLY:
        count = lax.axis_size(axis)
        if bit >= count:
            continue
        pairs = [(i, i ^ bit) for i in range(count)]
        value = combine(value, lax.ppermute(value, axis, pairs))
    return value


def butterfly_sum(parts):
    rows = [p.reshape(-1, 128) for p in parts]
    flat = butterfly(jnp.concatenate(rows, axis=0), lambda a, b: a + b)
    out, start = [], 0
    for p, r in zip(parts, rows):
        out.append(flat[start : start + r.shape[0]].reshape(p.shape))
        start += r.shape[0]
    return out


def pack_moments(n, mean, scat):
    groups, width = mean.shape
    count = jnp.broadcast_to(n.reshape(1, 1, 1), (groups, 1, width))
    pad = jnp.zeros((groups, 6, width), jnp.float32)
    return jnp.concatenate([scat, mean[:, None, :], count, pad], axis=1)


def unpack_moments(packed):
    width = packed.shape[2]
    return (packed[:, width + 1 : width + 2], packed[:, width : width + 1], packed[:, :width])


def merge_moments(a, b):
    width = a.shape[2]
    n_a, mean_a, _ = unpack_moments(a)
    n_b, mean_b, _ = unpack_moments(b)
    n = n_a + n_b
    mean = (n_a * mean_a + n_b * mean_b) / n
    delta = mean_b - mean_a
    column = jnp.pad(jnp.swapaxes(delta, 1, 2), ((0, 0), (0, a.shape[1] - width), (0, 0)))
    scat = (a + b) + (n_a * n_b / n) * (column * delta)
    rows = lax.broadcasted_iota(jnp.int32, a.shape, 1)
    fill = jnp.where(rows == width, mean, jnp.where(rows == width + 1, n, 0.0))
    return jnp.where(rows < width, scat, fill)


def whiten(sigma):
    eye = jnp.eye(sigma.shape[0], dtype=sigma.dtype)
    trace = jnp.trace(sigma)
    scaled = sigma / trace
    proj = eye
    for sweep in range(SWEEPS):
        cube = jnp.dot(
            proj, jnp.dot(proj, jnp.dot(proj, scaled, precision=HI), precision=HI), precision=HI
        )
        proj = 1.5 * proj - 0.5 * cube
    return proj / jnp.sqrt(trace)


def mm(a, b):
    return jnp.dot(a, b, precision=HI, preferred_element_type=jnp.float32)


def unit(width):
    rows = lax.broadcasted_iota(jnp.int32, (width, width), 0)
    cols = lax.broadcasted_iota(jnp.int32, (width, width), 1)
    return (rows == cols).astype(jnp.float32)


def whiten_fwd_kernel(sig_ref, white_ref, scaled_ref, ps_ref, as_ref, bs_ref):
    groups, width, _ = sig_ref.shape
    eye = unit(width)
    traces, scaled, proj = [], [], []
    for g in range(groups):
        sig = sig_ref[g]
        trace = jnp.sum(sig * eye, keepdims=True)
        traces.append(trace)
        scaled.append(sig / trace)
        scaled_ref[g] = scaled[g]
        proj.append(eye)
    for sweep in range(SWEEPS):
        first = [mm(proj[g], scaled[g]) for g in range(groups)]
        second = [mm(proj[g], first[g]) for g in range(groups)]
        cube = [mm(proj[g], second[g]) for g in range(groups)]
        for g in range(groups):
            ps_ref[g, sweep] = proj[g]
            as_ref[g, sweep] = first[g]
            bs_ref[g, sweep] = second[g]
            proj[g] = 1.5 * proj[g] - 0.5 * cube[g]
    for g in range(groups):
        ps_ref[g, SWEEPS] = proj[g]
        white_ref[g] = proj[g] / jnp.sqrt(traces[g])


def whiten_bwd_kernel(sig_ref, scaled_ref, ps_ref, as_ref, bs_ref, dwhite_ref, sens_ref):
    groups, width, _ = sig_ref.shape
    eye = unit(width)
    traces, roots, grad, grad_trace, grad_scaled = [], [], [], [], []
    for g in range(groups):
        sig = sig_ref[g]
        trace = jnp.sum(sig * eye, keepdims=True)
        root = jnp.sqrt(trace)
        dwhite = dwhite_ref[g]
        traces.append(trace)
        grad.append(dwhite / root)
        grad_trace.append(-0.5 * jnp.sum(dwhite * ps_ref[g, SWEEPS], keepdims=True) / (trace * root))
        grad_scaled.append(jnp.zeros_like(sig))
    for sweep in reversed(range(SWEEPS)):
        proj = [ps_ref[g, sweep] for g in range(groups)]
        grad_cube = [-0.5 * grad[g] for g in range(groups)]
        grad_second = [mm(proj[g], grad_cube[g]) for g in range(groups)]
        grad_first = [mm(proj[g], grad_second[g]) for g in range(groups)]
        for g in range(groups):
            grad_scaled[g] = grad_scaled[g] + mm(proj[g], grad_first[g])
            grad[g] = (
                1.5 * grad[g]
                + mm(grad_cube[g], bs_ref[g, sweep])
                + mm(grad_second[g], as_ref[g, sweep])
                + mm(grad_first[g], scaled_ref[g])
            )
    for g in range(groups):
        trace = traces[g]
        total = grad_trace[g] - jnp.sum(grad_scaled[g] * sig_ref[g], keepdims=True) / (trace * trace)
        sens_ref[g] = grad_scaled[g] / trace + total * eye


def whiten_fwd(sigma):
    groups, width, _ = sigma.shape
    f32 = jnp.float32
    return pl.pallas_call(
        whiten_fwd_kernel,
        out_shape=[
            jax.ShapeDtypeStruct((groups, width, width), f32),
            jax.ShapeDtypeStruct((groups, width, width), f32),
            jax.ShapeDtypeStruct((groups, SWEEPS + 1, width, width), f32),
            jax.ShapeDtypeStruct((groups, SWEEPS, width, width), f32),
            jax.ShapeDtypeStruct((groups, SWEEPS, width, width), f32),
        ],
    )(sigma)


def whiten_bwd(sigma, scaled, ps, as_, bs, dwhite):
    groups, width, _ = sigma.shape
    return pl.pallas_call(
        whiten_bwd_kernel,
        out_shape=jax.ShapeDtypeStruct((groups, width, width), jnp.float32),
    )(sigma, scaled, ps, as_, bs, dwhite)


def zwrap(field):
    return jnp.concatenate([field[:, :, -1:], field, field[:, :, :1]], axis=2)


def stencil(padded, kernel, flip):
    size_x, size_y, depth = (padded.shape[0] - 2, padded.shape[1] - 2, padded.shape[2] - 2)
    taps = kernel.astype(jnp.float32)
    total = jnp.zeros((size_x, size_y, depth, padded.shape[3]), jnp.float32)
    for tap in range(27):
        ox, oy, oz = (tap // 9, tap // 3 % 3, tap % 3)
        if flip:
            ox, oy, oz = (2 - ox, 2 - oy, 2 - oz)
        piece = padded[ox : ox + size_x, oy : oy + size_y, oz : oz + depth]
        total = total + piece.astype(jnp.float32) * taps[tap]
    return total


def inner(field, edge):
    return field[edge : field.shape[0] - edge, edge : field.shape[1] - edge]


def per_device(volume, void_mask, kernel, mix_weight, norm_gain, upstream):
    size_x, size_y, depth, chans = volume.shape
    groups, width = (mix_weight.shape[0], mix_weight.shape[1])
    scale = jnp.float32(size_x * size_y * depth * lax.axis_size("gx") * lax.axis_size("gy"))
    keep_own = (1 - void_mask).astype(jnp.float32)
    rim = 1
    padded_x = padded_2(volume, (("gx", 0), ("gy", 1)), 1)
    edge = rim - 1
    padded_z = zwrap(padded_x)
    field = lax.optimization_barrier(stencil(padded_z, kernel, False).astype(jnp.bfloat16)).astype(
        jnp.float32
    )
    ext_x, ext_y = (field.shape[0], field.shape[1])
    field_own = inner(field, edge)
    masked_own = keep_own[..., None] * field_own
    count_part = jnp.sum(keep_own)
    sum_part = jnp.sum(masked_own, axis=(0, 1, 2))
    eye = jnp.eye(width, dtype=jnp.float32)
    mean_part = (sum_part / count_part).reshape(groups, width)
    cent_part = field_own.reshape(size_x, size_y, depth, groups, width) - mean_part
    cov_part = jnp.einsum(
        "abzgi,abzgj->gij", keep_own[..., None, None] * cent_part, cent_part, precision=HI
    )
    moments = butterfly(pack_moments(count_part, mean_part, cov_part), merge_moments)
    count, mean, scatter = unpack_moments(moments)
    count = count[0, 0, 0]
    mean = mean[:, 0]
    sigma = scatter / count + EPS * eye
    white, scaled, ps, as_, bs = whiten_fwd(sigma)
    centered = field.reshape(ext_x, ext_y, depth, groups, width) - mean
    gain = norm_gain.reshape(groups, width)
    pre = jnp.einsum("abzgj,gij->abzgi", centered, white, precision=HI) * gain
    active = jax.nn.silu(pre).astype(jnp.bfloat16)
    active_own = inner(active, edge)
    grad_five = upstream.reshape(ext_x, ext_y, depth, groups, width)
    mixed = jnp.einsum(
        "abzgi,gio->abzgo", active_own, mix_weight, preferred_element_type=jnp.float32
    )
    output = (volume.astype(jnp.float32) + mixed.reshape(size_x, size_y, depth, chans)).astype(
        jnp.bfloat16
    )
    mix_part = jnp.einsum(
        "abzgi,abzgo->gio",
        active_own,
        upstream.reshape(size_x, size_y, depth, groups, width),
        preferred_element_type=jnp.float32,
    )
    dact = jnp.einsum("abzgo,gio->abzgi", grad_five, mix_weight, preferred_element_type=jnp.float32)
    sig = jax.nn.sigmoid(pre)
    dnormed = dact * sig * (1.0 + pre * (1.0 - sig)) * gain
    dcent = jnp.einsum("abzgi,gij->abzgj", dnormed, white, precision=HI)
    dwhite_part = jnp.einsum(
        "abzgi,abzgj->gij", inner(dnormed, edge), inner(centered, edge), precision=HI
    )
    dsum_part = jnp.sum(inner(dcent, edge), axis=(0, 1, 2))
    dwhite, dsum = butterfly_sum((dwhite_part, dsum_part))
    sens = whiten_bwd(sigma, scaled, ps, as_, bs, dwhite)
    sym = sens + jnp.swapaxes(sens, 1, 2)
    dfield = dcent + keep_own[..., None, None] / count * (
        jnp.einsum("abzgj,gjk->abzgk", centered, sym, precision=HI) - dsum
    )
    dfield = lax.optimization_barrier(
        dfield.astype(jnp.bfloat16).reshape(ext_x, ext_y, depth, chans)
    )
    dfield_pad = zwrap(padded_2(dfield, (("gx", 0), ("gy", 1)), 1))
    back = stencil(dfield_pad, kernel, True)
    volume_grad = (upstream.astype(jnp.float32) + back).astype(jnp.bfloat16)
    dfield_own = inner(dfield, edge).astype(jnp.float32)
    ker_terms = []
    for tap in range(27):
        ox, oy, oz = (tap // 9, tap // 3 % 3, tap % 3)
        piece = padded_z[
            edge + ox : edge + ox + size_x, edge + oy : edge + oy + size_y, oz : oz + depth
        ]
        ker_terms.append(jnp.sum(piece.astype(jnp.float32) * dfield_own, axis=(0, 1, 2)))
    ker_part = jnp.stack(ker_terms)
    ker_sum, mix_sum = butterfly_sum((ker_part, mix_part))
    return (output, volume_grad, ker_sum / scale, mix_sum / scale)


def solution(mesh):
    in_specs = (
        P("gx", "gy", None, None),
        P("gx", "gy", None),
        P(),
        P(),
        P(),
        P("gx", "gy", None, None),
    )
    out_specs = (P("gx", "gy", None, None), P("gx", "gy", None, None), P(), P())
    return jax.shard_map(
        per_device, mesh=mesh, in_specs=in_specs, out_specs=out_specs, check_vma=False
    )
```

```python
import jax
import jax.numpy as jnp
from jax import lax
from jax.experimental import pallas as pl
from jax.sharding import PartitionSpec as P

SWEEPS = 5


HI = lax.Precision.HIGHEST
EPS = 1e-05


def padded_2(block, sides, width):
    for axis, dim in sides:
        count = lax.axis_size(axis)
        forward = [(i, i + 1) for i in range(count - 1)]
        forward.append((count - 1, 0))
        backward = [(target, source) for source, target in forward]
        low = lax.ppermute(
            lax.slice_in_dim(block, block.shape[dim] - width, None, axis=dim), axis, forward
        )
        high = lax.ppermute(lax.slice_in_dim(block, 0, width, axis=dim), axis, backward)
        block = jnp.concatenate([low, block, high], axis=dim)
    return block


BUTTERFLY = (("gx", 1), ("gx", 2), ("gx", 4), ("gx", 8), ("gx", 16), ("gx", 32), ("gy", 1), ("gy", 2))


def butterfly(value, combine):
    for axis, bit in BUTTERFLY:
        count = lax.axis_size(axis)
        if bit >= count:
            continue
        pairs = [(i, i ^ bit) for i in range(count)]
        value = combine(value, lax.ppermute(value, axis, pairs))
    return value


def butterfly_sum(parts):
    rows = [p.reshape(-1, 128) for p in parts]
    flat = butterfly(jnp.concatenate(rows, axis=0), lambda a, b: a + b)
    out, start = [], 0
    for p, r in zip(parts, rows):
        out.append(flat[start : start + r.shape[0]].reshape(p.shape))
        start += r.shape[0]
    return out


def pack_moments(n, mean, scat):
    groups, width = mean.shape
    count = jnp.broadcast_to(n.reshape(1, 1, 1), (groups, 1, width))
    pad = jnp.zeros((groups, 6, width), jnp.float32)
    return jnp.concatenate([scat, mean[:, None, :], count, pad], axis=1)


def unpack_moments(packed):
    width = packed.shape[2]
    return (packed[:, width + 1 : width + 2], packed[:, width : width + 1], packed[:, :width])


def merge_moments(a, b):
    width = a.shape[2]
    n_a, mean_a, _ = unpack_moments(a)
    n_b, mean_b, _ = unpack_moments(b)
    n = n_a + n_b
    mean = (n_a * mean_a + n_b * mean_b) / n
    delta = mean_b - mean_a
    column = jnp.pad(jnp.swapaxes(delta, 1, 2), ((0, 0), (0, a.shape[1] - width), (0, 0)))
    scat = (a + b) + (n_a * n_b / n) * (column * delta)
    rows = lax.broadcasted_iota(jnp.int32, a.shape, 1)
    fill = jnp.where(rows == width, mean, jnp.where(rows == width + 1, n, 0.0))
    return jnp.where(rows < width, scat, fill)


def whiten(sigma):
    eye = jnp.eye(sigma.shape[0], dtype=sigma.dtype)
    trace = jnp.trace(sigma)
    scaled = sigma / trace
    proj = eye
    for sweep in range(SWEEPS):
        cube = jnp.dot(
            proj, jnp.dot(proj, jnp.dot(proj, scaled, precision=HI), precision=HI), precision=HI
        )
        proj = 1.5 * proj - 0.5 * cube
    return proj / jnp.sqrt(trace)


def mm(a, b):
    return jnp.dot(a, b, precision=HI, preferred_element_type=jnp.float32)


def unit(width):
    rows = lax.broadcasted_iota(jnp.int32, (width, width), 0)
    cols = lax.broadcasted_iota(jnp.int32, (width, width), 1)
    return (rows == cols).astype(jnp.float32)


def whiten_fwd_kernel(sig_ref, white_ref, scaled_ref, ps_ref, as_ref, bs_ref):
    groups, width, _ = sig_ref.shape
    eye = unit(width)
    traces, scaled, proj = [], [], []
    for g in range(groups):
        sig = sig_ref[g]
        trace = jnp.sum(sig * eye, keepdims=True)
        traces.append(trace)
        scaled.append(sig / trace)
        scaled_ref[g] = scaled[g]
        proj.append(eye)

    def sweep_step(sweep, proj):
        first = [mm(proj[g], scaled[g]) for g in range(groups)]
        second = [mm(proj[g], first[g]) for g in range(groups)]
        cube = [mm(proj[g], second[g]) for g in range(groups)]
        for g in range(groups):
            ps_ref[g, sweep] = proj[g]
            as_ref[g, sweep] = first[g]
            bs_ref[g, sweep] = second[g]
        return [1.5 * proj[g] - 0.5 * cube[g] for g in range(groups)]

    proj = lax.fori_loop(0, SWEEPS, sweep_step, proj)
    for g in range(groups):
        ps_ref[g, SWEEPS] = proj[g]
        white_ref[g] = proj[g] / jnp.sqrt(traces[g])


def whiten_bwd_kernel(sig_ref, scaled_ref, ps_ref, as_ref, bs_ref, dwhite_ref, sens_ref):
    groups, width, _ = sig_ref.shape
    eye = unit(width)
    traces, roots, grad, grad_trace, grad_scaled = [], [], [], [], []
    for g in range(groups):
        sig = sig_ref[g]
        trace = jnp.sum(sig * eye, keepdims=True)
        root = jnp.sqrt(trace)
        dwhite = dwhite_ref[g]
        traces.append(trace)
        grad.append(dwhite / root)
        grad_trace.append(-0.5 * jnp.sum(dwhite * ps_ref[g, SWEEPS], keepdims=True) / (trace * root))
        grad_scaled.append(jnp.zeros_like(sig))

    def sweep_step(step, carry):
        grad, grad_scaled = carry
        sweep = SWEEPS - 1 - step
        proj = [ps_ref[g, sweep] for g in range(groups)]
        grad_cube = [-0.5 * grad[g] for g in range(groups)]
        grad_second = [mm(proj[g], grad_cube[g]) for g in range(groups)]
        grad_first = [mm(proj[g], grad_second[g]) for g in range(groups)]
        new_scaled, new_grad = [], []
        for g in range(groups):
            new_scaled.append(grad_scaled[g] + mm(proj[g], grad_first[g]))
            new_grad.append(
                1.5 * grad[g]
                + mm(grad_cube[g], bs_ref[g, sweep])
                + mm(grad_second[g], as_ref[g, sweep])
                + mm(grad_first[g], scaled_ref[g])
            )
        return (new_grad, new_scaled)

    grad, grad_scaled = lax.fori_loop(0, SWEEPS, sweep_step, (grad, grad_scaled))
    for g in range(groups):
        trace = traces[g]
        total = grad_trace[g] - jnp.sum(grad_scaled[g] * sig_ref[g], keepdims=True) / (trace * trace)
        sens_ref[g] = grad_scaled[g] / trace + total * eye


def whiten_fwd(sigma):
    groups, width, _ = sigma.shape
    f32 = jnp.float32
    return pl.pallas_call(
        whiten_fwd_kernel,
        out_shape=[
            jax.ShapeDtypeStruct((groups, width, width), f32),
            jax.ShapeDtypeStruct((groups, width, width), f32),
            jax.ShapeDtypeStruct((groups, SWEEPS + 1, width, width), f32),
            jax.ShapeDtypeStruct((groups, SWEEPS, width, width), f32),
            jax.ShapeDtypeStruct((groups, SWEEPS, width, width), f32),
        ],
    )(sigma)


def whiten_bwd(sigma, scaled, ps, as_, bs, dwhite):
    groups, width, _ = sigma.shape
    return pl.pallas_call(
        whiten_bwd_kernel,
        out_shape=jax.ShapeDtypeStruct((groups, width, width), jnp.float32),
    )(sigma, scaled, ps, as_, bs, dwhite)


def zwrap(field):
    return jnp.concatenate([field[:, :, -1:], field, field[:, :, :1]], axis=2)


def stencil(padded, kernel, flip):
    size_x, size_y, depth = (padded.shape[0] - 2, padded.shape[1] - 2, padded.shape[2] - 2)
    taps = kernel.astype(jnp.float32)
    total = jnp.zeros((size_x, size_y, depth, padded.shape[3]), jnp.float32)
    for tap in range(27):
        ox, oy, oz = (tap // 9, tap // 3 % 3, tap % 3)
        if flip:
            ox, oy, oz = (2 - ox, 2 - oy, 2 - oz)
        piece = padded[ox : ox + size_x, oy : oy + size_y, oz : oz + depth]
        total = total + piece.astype(jnp.float32) * taps[tap]
    return total


def inner(field, edge):
    return field[edge : field.shape[0] - edge, edge : field.shape[1] - edge]


def per_device(volume, void_mask, kernel, mix_weight, norm_gain, upstream):
    size_x, size_y, depth, chans = volume.shape
    groups, width = (mix_weight.shape[0], mix_weight.shape[1])
    scale = jnp.float32(size_x * size_y * depth * lax.axis_size("gx") * lax.axis_size("gy"))
    keep_own = (1 - void_mask).astype(jnp.float32)
    rim = 1
    padded_x = padded_2(volume, (("gx", 0), ("gy", 1)), 1)
    edge = rim - 1
    padded_z = zwrap(padded_x)
    field = lax.optimization_barrier(stencil(padded_z, kernel, False).astype(jnp.bfloat16)).astype(
        jnp.float32
    )
    ext_x, ext_y = (field.shape[0], field.shape[1])
    field_own = inner(field, edge)
    masked_own = keep_own[..., None] * field_own
    count_part = jnp.sum(keep_own)
    sum_part = jnp.sum(masked_own, axis=(0, 1, 2))
    eye = jnp.eye(width, dtype=jnp.float32)
    mean_part = (sum_part / count_part).reshape(groups, width)
    cent_part = field_own.reshape(size_x, size_y, depth, groups, width) - mean_part
    cov_part = jnp.einsum(
        "abzgi,abzgj->gij", keep_own[..., None, None] * cent_part, cent_part, precision=HI
    )
    moments = butterfly(pack_moments(count_part, mean_part, cov_part), merge_moments)
    count, mean, scatter = unpack_moments(moments)
    count = count[0, 0, 0]
    mean = mean[:, 0]
    sigma = scatter / count + EPS * eye
    white, scaled, ps, as_, bs = whiten_fwd(sigma)
    centered = field.reshape(ext_x, ext_y, depth, groups, width) - mean
    gain = norm_gain.reshape(groups, width)
    pre = jnp.einsum("abzgj,gij->abzgi", centered, white, precision=HI) * gain
    active = jax.nn.silu(pre).astype(jnp.bfloat16)
    active_own = inner(active, edge)
    grad_five = upstream.reshape(ext_x, ext_y, depth, groups, width)
    mixed = jnp.einsum(
        "abzgi,gio->abzgo", active_own, mix_weight, preferred_element_type=jnp.float32
    )
    output = (volume.astype(jnp.float32) + mixed.reshape(size_x, size_y, depth, chans)).astype(
        jnp.bfloat16
    )
    mix_part = jnp.einsum(
        "abzgi,abzgo->gio",
        active_own,
        upstream.reshape(size_x, size_y, depth, groups, width),
        preferred_element_type=jnp.float32,
    )
    dact = jnp.einsum("abzgo,gio->abzgi", grad_five, mix_weight, preferred_element_type=jnp.float32)
    sig = jax.nn.sigmoid(pre)
    dnormed = dact * sig * (1.0 + pre * (1.0 - sig)) * gain
    dcent = jnp.einsum("abzgi,gij->abzgj", dnormed, white, precision=HI)
    dwhite_part = jnp.einsum(
        "abzgi,abzgj->gij", inner(dnormed, edge), inner(centered, edge), precision=HI
    )
    dsum_part = jnp.sum(inner(dcent, edge), axis=(0, 1, 2))
    dwhite, dsum = butterfly_sum((dwhite_part, dsum_part))
    sens = whiten_bwd(sigma, scaled, ps, as_, bs, dwhite)
    sym = sens + jnp.swapaxes(sens, 1, 2)
    dfield = dcent + keep_own[..., None, None] / count * (
        jnp.einsum("abzgj,gjk->abzgk", centered, sym, precision=HI) - dsum
    )
    dfield = lax.optimization_barrier(
        dfield.astype(jnp.bfloat16).reshape(ext_x, ext_y, depth, chans)
    )
    dfield_pad = zwrap(padded_2(dfield, (("gx", 0), ("gy", 1)), 1))
    back = stencil(dfield_pad, kernel, True)
    volume_grad = (upstream.astype(jnp.float32) + back).astype(jnp.bfloat16)
    dfield_own = inner(dfield, edge).astype(jnp.float32)
    ker_terms = []
    for tap in range(27):
        ox, oy, oz = (tap // 9, tap // 3 % 3, tap % 3)
        piece = padded_z[
            edge + ox : edge + ox + size_x, edge + oy : edge + oy + size_y, oz : oz + depth
        ]
        ker_terms.append(jnp.sum(piece.astype(jnp.float32) * dfield_own, axis=(0, 1, 2)))
    ker_part = jnp.stack(ker_terms)
    ker_sum, mix_sum = butterfly_sum((ker_part, mix_part))
    return (output, volume_grad, ker_sum / scale, mix_sum / scale)


def solution(mesh):
    in_specs = (
        P("gx", "gy", None, None),
        P("gx", "gy", None),
        P(),
        P(),
        P(),
        P("gx", "gy", None, None),
    )
    out_specs = (P("gx", "gy", None, None), P("gx", "gy", None, None), P(), P())
    return jax.shard_map(
        per_device, mesh=mesh, in_specs=in_specs, out_specs=out_specs, check_vma=False
    )
```

```python
import jax
import jax.numpy as jnp
from jax import lax
from jax.experimental import pallas as pl
from jax.sharding import PartitionSpec as P

SWEEPS = 5


HI = lax.Precision.HIGHEST
EPS = 1e-05


def padded_2(block, sides, width):
    for axis, dim in sides:
        count = lax.axis_size(axis)
        forward = [(i, i + 1) for i in range(count - 1)]
        forward.append((count - 1, 0))
        backward = [(target, source) for source, target in forward]
        low = lax.ppermute(
            lax.slice_in_dim(block, block.shape[dim] - width, None, axis=dim), axis, forward
        )
        high = lax.ppermute(lax.slice_in_dim(block, 0, width, axis=dim), axis, backward)
        block = jnp.concatenate([low, block, high], axis=dim)
    return block


BUTTERFLY = (("gx", 1), ("gx", 2), ("gx", 4), ("gx", 8), ("gx", 16), ("gx", 32), ("gy", 1), ("gy", 2))


def butterfly(value, combine):
    for axis, bit in BUTTERFLY:
        count = lax.axis_size(axis)
        if bit >= count:
            continue
        pairs = [(i, i ^ bit) for i in range(count)]
        value = combine(value, lax.ppermute(value, axis, pairs))
    return value


def butterfly_sum(parts):
    rows = [p.reshape(-1, 128) for p in parts]
    flat = butterfly(jnp.concatenate(rows, axis=0), lambda a, b: a + b)
    out, start = [], 0
    for p, r in zip(parts, rows):
        out.append(flat[start : start + r.shape[0]].reshape(p.shape))
        start += r.shape[0]
    return out


def pack_moments(n, mean, scat):
    groups, width = mean.shape
    count = jnp.broadcast_to(n.reshape(1, 1, 1), (groups, 1, width))
    return jnp.concatenate([scat, mean[:, None, :], count], axis=1)


def unpack_moments(packed):
    width = packed.shape[2]
    return (packed[:, width + 1 : width + 2], packed[:, width : width + 1], packed[:, :width])


def merge_moments(a, b):
    width = a.shape[2]
    n_a, mean_a, _ = unpack_moments(a)
    n_b, mean_b, _ = unpack_moments(b)
    n = n_a + n_b
    mean = (n_a * mean_a + n_b * mean_b) / n
    delta = mean_b - mean_a
    column = jnp.pad(jnp.swapaxes(delta, 1, 2), ((0, 0), (0, a.shape[1] - width), (0, 0)))
    scat = (a + b) + (n_a * n_b / n) * (column * delta)
    rows = lax.broadcasted_iota(jnp.int32, a.shape, 1)
    fill = jnp.where(rows == width, mean, jnp.where(rows == width + 1, n, 0.0))
    return jnp.where(rows < width, scat, fill)


def whiten(sigma):
    eye = jnp.eye(sigma.shape[0], dtype=sigma.dtype)
    trace = jnp.trace(sigma)
    scaled = sigma / trace
    proj = eye
    for sweep in range(SWEEPS):
        cube = jnp.dot(
            proj, jnp.dot(proj, jnp.dot(proj, scaled, precision=HI), precision=HI), precision=HI
        )
        proj = 1.5 * proj - 0.5 * cube
    return proj / jnp.sqrt(trace)


def mm(a, b):
    return jnp.dot(a, b, precision=HI, preferred_element_type=jnp.float32)


def unit(width):
    rows = lax.broadcasted_iota(jnp.int32, (width, width), 0)
    cols = lax.broadcasted_iota(jnp.int32, (width, width), 1)
    return (rows == cols).astype(jnp.float32)


def whiten_fwd_kernel(sig_ref, white_ref, scaled_ref, ps_ref, as_ref, bs_ref):
    groups, width, _ = sig_ref.shape
    eye = unit(width)
    traces, scaled, proj = [], [], []
    for g in range(groups):
        sig = sig_ref[g]
        trace = jnp.sum(sig * eye, keepdims=True)
        traces.append(trace)
        scaled.append(sig / trace)
        scaled_ref[g] = scaled[g]
        proj.append(eye)
    for sweep in range(SWEEPS):
        first = [mm(proj[g], scaled[g]) for g in range(groups)]
        second = [mm(proj[g], first[g]) for g in range(groups)]
        cube = [mm(proj[g], second[g]) for g in range(groups)]
        for g in range(groups):
            ps_ref[g, sweep] = proj[g]
            as_ref[g, sweep] = first[g]
            bs_ref[g, sweep] = second[g]
            proj[g] = 1.5 * proj[g] - 0.5 * cube[g]
    for g in range(groups):
        ps_ref[g, SWEEPS] = proj[g]
        white_ref[g] = proj[g] / jnp.sqrt(traces[g])


def whiten_bwd_kernel(sig_ref, scaled_ref, ps_ref, as_ref, bs_ref, dwhite_ref, sens_ref):
    groups, width, _ = sig_ref.shape
    eye = unit(width)
    traces, roots, grad, grad_trace, grad_scaled = [], [], [], [], []
    for g in range(groups):
        sig = sig_ref[g]
        trace = jnp.sum(sig * eye, keepdims=True)
        root = jnp.sqrt(trace)
        dwhite = dwhite_ref[g]
        traces.append(trace)
        grad.append(dwhite / root)
        grad_trace.append(-0.5 * jnp.sum(dwhite * ps_ref[g, SWEEPS], keepdims=True) / (trace * root))
        grad_scaled.append(jnp.zeros_like(sig))
    for sweep in reversed(range(SWEEPS)):
        proj = [ps_ref[g, sweep] for g in range(groups)]
        grad_cube = [-0.5 * grad[g] for g in range(groups)]
        grad_second = [mm(proj[g], grad_cube[g]) for g in range(groups)]
        grad_first = [mm(proj[g], grad_second[g]) for g in range(groups)]
        for g in range(groups):
            grad_scaled[g] = grad_scaled[g] + mm(proj[g], grad_first[g])
            grad[g] = (
                1.5 * grad[g]
                + mm(grad_cube[g], bs_ref[g, sweep])
                + mm(grad_second[g], as_ref[g, sweep])
                + mm(grad_first[g], scaled_ref[g])
            )
    for g in range(groups):
        trace = traces[g]
        total = grad_trace[g] - jnp.sum(grad_scaled[g] * sig_ref[g], keepdims=True) / (trace * trace)
        sens_ref[g] = grad_scaled[g] / trace + total * eye


def whiten_fwd(sigma):
    groups, width, _ = sigma.shape
    f32 = jnp.float32
    return pl.pallas_call(
        whiten_fwd_kernel,
        out_shape=[
            jax.ShapeDtypeStruct((groups, width, width), f32),
            jax.ShapeDtypeStruct((groups, width, width), f32),
            jax.ShapeDtypeStruct((groups, SWEEPS + 1, width, width), f32),
            jax.ShapeDtypeStruct((groups, SWEEPS, width, width), f32),
            jax.ShapeDtypeStruct((groups, SWEEPS, width, width), f32),
        ],
    )(sigma)


def whiten_bwd(sigma, scaled, ps, as_, bs, dwhite):
    groups, width, _ = sigma.shape
    return pl.pallas_call(
        whiten_bwd_kernel,
        out_shape=jax.ShapeDtypeStruct((groups, width, width), jnp.float32),
    )(sigma, scaled, ps, as_, bs, dwhite)


def zwrap(field):
    return jnp.concatenate([field[:, :, -1:], field, field[:, :, :1]], axis=2)


def stencil(padded, kernel, flip):
    size_x, size_y, depth = (padded.shape[0] - 2, padded.shape[1] - 2, padded.shape[2] - 2)
    taps = kernel.astype(jnp.float32)
    total = jnp.zeros((size_x, size_y, depth, padded.shape[3]), jnp.float32)
    for tap in range(27):
        ox, oy, oz = (tap // 9, tap // 3 % 3, tap % 3)
        if flip:
            ox, oy, oz = (2 - ox, 2 - oy, 2 - oz)
        piece = padded[ox : ox + size_x, oy : oy + size_y, oz : oz + depth]
        total = total + piece.astype(jnp.float32) * taps[tap]
    return total


def inner(field, edge):
    return field[edge : field.shape[0] - edge, edge : field.shape[1] - edge]


def per_device(volume, void_mask, kernel, mix_weight, norm_gain, upstream):
    size_x, size_y, depth, chans = volume.shape
    groups, width = (mix_weight.shape[0], mix_weight.shape[1])
    scale = jnp.float32(size_x * size_y * depth * lax.axis_size("gx") * lax.axis_size("gy"))
    keep_own = (1 - void_mask).astype(jnp.float32)
    rim = 1
    padded_x = padded_2(volume, (("gx", 0), ("gy", 1)), 1)
    edge = rim - 1
    padded_z = zwrap(padded_x)
    field = lax.optimization_barrier(stencil(padded_z, kernel, False).astype(jnp.bfloat16)).astype(
        jnp.float32
    )
    ext_x, ext_y = (field.shape[0], field.shape[1])
    field_own = inner(field, edge)
    masked_own = keep_own[..., None] * field_own
    count_part = jnp.sum(keep_own)
    sum_part = jnp.sum(masked_own, axis=(0, 1, 2))
    eye = jnp.eye(width, dtype=jnp.float32)
    mean_part = (sum_part / count_part).reshape(groups, width)
    cent_part = field_own.reshape(size_x, size_y, depth, groups, width) - mean_part
    cov_part = jnp.einsum(
        "abzgi,abzgj->gij", keep_own[..., None, None] * cent_part, cent_part, precision=HI
    )
    moments = butterfly(pack_moments(count_part, mean_part, cov_part), merge_moments)
    count, mean, scatter = unpack_moments(moments)
    count = count[0, 0, 0]
    mean = mean[:, 0]
    sigma = scatter / count + EPS * eye
    white, scaled, ps, as_, bs = whiten_fwd(sigma)
    centered = field.reshape(ext_x, ext_y, depth, groups, width) - mean
    gain = norm_gain.reshape(groups, width)
    pre = jnp.einsum("abzgj,gij->abzgi", centered, white, precision=HI) * gain
    active = jax.nn.silu(pre).astype(jnp.bfloat16)
    active_own = inner(active, edge)
    grad_five = upstream.reshape(ext_x, ext_y, depth, groups, width)
    mixed = jnp.einsum(
        "abzgi,gio->abzgo", active_own, mix_weight, preferred_element_type=jnp.float32
    )
    output = (volume.astype(jnp.float32) + mixed.reshape(size_x, size_y, depth, chans)).astype(
        jnp.bfloat16
    )
    mix_part = jnp.einsum(
        "abzgi,abzgo->gio",
        active_own,
        upstream.reshape(size_x, size_y, depth, groups, width),
        preferred_element_type=jnp.float32,
    )
    dact = jnp.einsum("abzgo,gio->abzgi", grad_five, mix_weight, preferred_element_type=jnp.float32)
    sig = jax.nn.sigmoid(pre)
    dnormed = dact * sig * (1.0 + pre * (1.0 - sig)) * gain
    dcent = jnp.einsum("abzgi,gij->abzgj", dnormed, white, precision=HI)
    dwhite_part = jnp.einsum(
        "abzgi,abzgj->gij", inner(dnormed, edge), inner(centered, edge), precision=HI
    )
    dsum_part = jnp.sum(inner(dcent, edge), axis=(0, 1, 2))
    dwhite, dsum = butterfly_sum((dwhite_part, dsum_part))
    sens = whiten_bwd(sigma, scaled, ps, as_, bs, dwhite)
    sym = sens + jnp.swapaxes(sens, 1, 2)
    dfield = dcent + keep_own[..., None, None] / count * (
        jnp.einsum("abzgj,gjk->abzgk", centered, sym, precision=HI) - dsum
    )
    dfield = lax.optimization_barrier(
        dfield.astype(jnp.bfloat16).reshape(ext_x, ext_y, depth, chans)
    )
    dfield_pad = zwrap(padded_2(dfield, (("gx", 0), ("gy", 1)), 1))
    back = stencil(dfield_pad, kernel, True)
    volume_grad = (upstream.astype(jnp.float32) + back).astype(jnp.bfloat16)
    dfield_own = inner(dfield, edge).astype(jnp.float32)
    ker_terms = []
    for tap in range(27):
        ox, oy, oz = (tap // 9, tap // 3 % 3, tap % 3)
        piece = padded_z[
            edge + ox : edge + ox + size_x, edge + oy : edge + oy + size_y, oz : oz + depth
        ]
        ker_terms.append(jnp.sum(piece.astype(jnp.float32) * dfield_own, axis=(0, 1, 2)))
    ker_part = jnp.stack(ker_terms)
    ker_sum, mix_sum = butterfly_sum((ker_part, mix_part))
    return (output, volume_grad, ker_sum / scale, mix_sum / scale)


def solution(mesh):
    in_specs = (
        P("gx", "gy", None, None),
        P("gx", "gy", None),
        P(),
        P(),
        P(),
        P("gx", "gy", None, None),
    )
    out_specs = (P("gx", "gy", None, None), P("gx", "gy", None, None), P(), P())
    return jax.shard_map(
        per_device, mesh=mesh, in_specs=in_specs, out_specs=out_specs, check_vma=False
    )
```

```python
import jax
import jax.numpy as jnp
from jax import lax
from jax.experimental import pallas as pl
from jax.sharding import PartitionSpec as P

SWEEPS = 5


HI = lax.Precision.HIGHEST
EPS = 1e-05


def padded_2(block, sides, width):
    for axis, dim in sides:
        count = lax.axis_size(axis)
        forward = [(i, i + 1) for i in range(count - 1)]
        forward.append((count - 1, 0))
        backward = [(target, source) for source, target in forward]
        low = lax.ppermute(
            lax.slice_in_dim(block, block.shape[dim] - width, None, axis=dim), axis, forward
        )
        high = lax.ppermute(lax.slice_in_dim(block, 0, width, axis=dim), axis, backward)
        block = jnp.concatenate([low, block, high], axis=dim)
    return block


BUTTERFLY = (("gx", 1), ("gx", 2), ("gx", 4), ("gx", 8), ("gx", 16), ("gx", 32), ("gy", 1), ("gy", 2))


def butterfly(value, combine):
    for axis, bit in BUTTERFLY:
        count = lax.axis_size(axis)
        if bit >= count:
            continue
        pairs = [(i, i ^ bit) for i in range(count)]
        value = combine(value, lax.ppermute(value, axis, pairs))
    return value


def butterfly_sum(parts):
    rows = [p.reshape(-1, 128) for p in parts]
    flat = butterfly(jnp.concatenate(rows, axis=0), lambda a, b: a + b)
    out, start = [], 0
    for p, r in zip(parts, rows):
        out.append(flat[start : start + r.shape[0]].reshape(p.shape))
        start += r.shape[0]
    return out


def pack_moments(n, mean, scat):
    groups, width = mean.shape
    count = jnp.broadcast_to(n.reshape(1, 1, 1), (groups, 1, width))
    return jnp.concatenate([scat, mean[:, None, :], count], axis=1)


def unpack_moments(packed):
    width = packed.shape[2]
    return (packed[:, width + 1 : width + 2], packed[:, width : width + 1], packed[:, :width])


def merge_moments(a, b):
    width = a.shape[2]
    n_a, mean_a, _ = unpack_moments(a)
    n_b, mean_b, _ = unpack_moments(b)
    n = n_a + n_b
    mean = (n_a * mean_a + n_b * mean_b) / n
    delta = mean_b - mean_a
    column = jnp.pad(jnp.swapaxes(delta, 1, 2), ((0, 0), (0, a.shape[1] - width), (0, 0)))
    scat = (a + b) + (n_a * n_b / n) * (column * delta)
    rows = lax.broadcasted_iota(jnp.int32, a.shape, 1)
    fill = jnp.where(rows == width, mean, jnp.where(rows == width + 1, n, 0.0))
    return jnp.where(rows < width, scat, fill)


def whiten(sigma):
    eye = jnp.eye(sigma.shape[0], dtype=sigma.dtype)
    trace = jnp.trace(sigma)
    scaled = sigma / trace
    proj = eye
    for sweep in range(SWEEPS):
        cube = jnp.dot(
            proj, jnp.dot(proj, jnp.dot(proj, scaled, precision=HI), precision=HI), precision=HI
        )
        proj = 1.5 * proj - 0.5 * cube
    return proj / jnp.sqrt(trace)


def mm(a, b):
    return jnp.dot(a, b, precision=HI, preferred_element_type=jnp.float32)


def unit(width):
    rows = lax.broadcasted_iota(jnp.int32, (width, width), 0)
    cols = lax.broadcasted_iota(jnp.int32, (width, width), 1)
    return (rows == cols).astype(jnp.float32)


def whiten_fwd_kernel(sig_ref, white_ref, scaled_ref, ps_ref, as_ref, bs_ref):
    groups, width, _ = sig_ref.shape
    eye = unit(width)
    traces, scaled, proj = [], [], []
    for g in range(groups):
        sig = sig_ref[g]
        trace = jnp.sum(sig * eye, keepdims=True)
        traces.append(trace)
        scaled.append(sig / trace)
        scaled_ref[g] = scaled[g]
        proj.append(eye)
    for sweep in range(SWEEPS):
        first = [mm(proj[g], scaled[g]) for g in range(groups)]
        second = [mm(proj[g], first[g]) for g in range(groups)]
        cube = [mm(proj[g], second[g]) for g in range(groups)]
        for g in range(groups):
            ps_ref[g, sweep] = proj[g]
            as_ref[g, sweep] = first[g]
            bs_ref[g, sweep] = second[g]
            proj[g] = 1.5 * proj[g] - 0.5 * cube[g]
    for g in range(groups):
        ps_ref[g, SWEEPS] = proj[g]
        white_ref[g] = proj[g] / jnp.sqrt(traces[g])


def whiten_bwd_kernel(sig_ref, scaled_ref, ps_ref, as_ref, bs_ref, dwhite_ref, sens_ref):
    groups, width, _ = sig_ref.shape
    eye = unit(width)
    traces, roots, grad, grad_trace, grad_scaled = [], [], [], [], []
    for g in range(groups):
        sig = sig_ref[g]
        trace = jnp.sum(sig * eye, keepdims=True)
        root = jnp.sqrt(trace)
        dwhite = dwhite_ref[g]
        traces.append(trace)
        grad.append(dwhite / root)
        grad_trace.append(-0.5 * jnp.sum(dwhite * ps_ref[g, SWEEPS], keepdims=True) / (trace * root))
        grad_scaled.append(jnp.zeros_like(sig))
    for sweep in reversed(range(SWEEPS)):
        proj = [ps_ref[g, sweep] for g in range(groups)]
        grad_cube = [-0.5 * grad[g] for g in range(groups)]
        grad_second = [mm(proj[g], grad_cube[g]) for g in range(groups)]
        grad_first = [mm(proj[g], grad_second[g]) for g in range(groups)]
        for g in range(groups):
            grad_scaled[g] = grad_scaled[g] + mm(proj[g], grad_first[g])
            grad[g] = (
                1.5 * grad[g]
                + mm(grad_cube[g], bs_ref[g, sweep])
                + mm(grad_second[g], as_ref[g, sweep])
                + mm(grad_first[g], scaled_ref[g])
            )
    for g in range(groups):
        trace = traces[g]
        total = grad_trace[g] - jnp.sum(grad_scaled[g] * sig_ref[g], keepdims=True) / (trace * trace)
        sens_ref[g] = grad_scaled[g] / trace + total * eye


def whiten_fwd(sigma):
    groups, width, _ = sigma.shape
    f32 = jnp.float32
    return pl.pallas_call(
        whiten_fwd_kernel,
        out_shape=[
            jax.ShapeDtypeStruct((groups, width, width), f32),
            jax.ShapeDtypeStruct((groups, width, width), f32),
            jax.ShapeDtypeStruct((groups, SWEEPS + 1, width, width), f32),
            jax.ShapeDtypeStruct((groups, SWEEPS, width, width), f32),
            jax.ShapeDtypeStruct((groups, SWEEPS, width, width), f32),
        ],
    )(sigma)


def whiten_bwd(sigma, scaled, ps, as_, bs, dwhite):
    groups, width, _ = sigma.shape
    return pl.pallas_call(
        whiten_bwd_kernel,
        out_shape=jax.ShapeDtypeStruct((groups, width, width), jnp.float32),
    )(sigma, scaled, ps, as_, bs, dwhite)


def zwrap(field):
    return jnp.concatenate([field[:, :, -1:], field, field[:, :, :1]], axis=2)


def stencil(padded, kernel, flip):
    size_x, size_y, depth = (padded.shape[0] - 2, padded.shape[1] - 2, padded.shape[2] - 2)
    taps = kernel.astype(jnp.float32)
    total = jnp.zeros((size_x, size_y, depth, padded.shape[3]), jnp.float32)
    for tap in range(27):
        ox, oy, oz = (tap // 9, tap // 3 % 3, tap % 3)
        if flip:
            ox, oy, oz = (2 - ox, 2 - oy, 2 - oz)
        piece = padded[ox : ox + size_x, oy : oy + size_y, oz : oz + depth]
        total = total + piece.astype(jnp.float32) * taps[tap]
    return total


def inner(field, edge):
    return field[edge : field.shape[0] - edge, edge : field.shape[1] - edge]


def per_device(volume, void_mask, kernel, mix_weight, norm_gain, upstream):
    size_x, size_y, depth, chans = volume.shape
    groups, width = (mix_weight.shape[0], mix_weight.shape[1])
    scale = jnp.float32(size_x * size_y * depth * lax.axis_size("gx") * lax.axis_size("gy"))
    keep_own = (1 - void_mask).astype(jnp.float32)
    rim = 1
    padded_x = padded_2(volume, (("gx", 0), ("gy", 1)), 1)
    edge = rim - 1
    padded_z = zwrap(padded_x)
    field = lax.optimization_barrier(stencil(padded_z, kernel, False).astype(jnp.bfloat16)).astype(
        jnp.float32
    )
    ext_x, ext_y = (field.shape[0], field.shape[1])
    field_own = inner(field, edge)
    masked_own = keep_own[..., None] * field_own
    count_part = jnp.sum(keep_own)
    sum_part = jnp.sum(masked_own, axis=(0, 1, 2))
    eye = jnp.eye(width, dtype=jnp.float32)
    mean_part = (sum_part / count_part).reshape(groups, width)
    cent_part = field_own.reshape(size_x, size_y, depth, groups, width) - mean_part
    cov_part = jnp.einsum(
        "abzgi,abzgj->gij", keep_own[..., None, None] * cent_part, cent_part, precision=HI
    )
    moments = butterfly(pack_moments(count_part, mean_part, cov_part), merge_moments)
    count, mean, scatter = unpack_moments(moments)
    count = count[0, 0, 0]
    mean = mean[:, 0]
    sigma = scatter / count + EPS * eye
    white, scaled, ps, as_, bs = whiten_fwd(sigma)
    centered = field.reshape(ext_x, ext_y, depth, groups, width) - mean
    gain = norm_gain.reshape(groups, width)
    pre = jnp.einsum("abzgj,gij->abzgi", centered, white, precision=HI) * gain
    active = jax.nn.silu(pre).astype(jnp.bfloat16)
    active_own = inner(active, edge)
    grad_five = upstream.reshape(ext_x, ext_y, depth, groups, width)
    mixed = jnp.einsum(
        "abzgi,gio->abzgo", active_own, mix_weight, preferred_element_type=jnp.float32
    )
    output = (volume.astype(jnp.float32) + mixed.reshape(size_x, size_y, depth, chans)).astype(
        jnp.bfloat16
    )
    mix_part = jnp.einsum(
        "abzgi,abzgo->gio",
        active_own,
        upstream.reshape(size_x, size_y, depth, groups, width),
        preferred_element_type=jnp.float32,
    )
    dact = jnp.einsum("abzgo,gio->abzgi", grad_five, mix_weight, preferred_element_type=jnp.float32)
    sig = jax.nn.sigmoid(pre)
    dnormed = dact * sig * (1.0 + pre * (1.0 - sig)) * gain
    dcent = jnp.einsum("abzgi,gij->abzgj", dnormed, white, precision=HI)
    dwhite_part = jnp.einsum(
        "abzgi,abzgj->gij", inner(dnormed, edge), inner(centered, edge), precision=HI
    )
    dsum_part = jnp.sum(inner(dcent, edge), axis=(0, 1, 2))
    dwhite, dsum = butterfly_sum((dwhite_part, dsum_part))
    sens = whiten_bwd(sigma, scaled, ps, as_, bs, dwhite)
    sym = sens + jnp.swapaxes(sens, 1, 2)
    dfield = dcent + keep_own[..., None, None] / count * (
        jnp.einsum("abzgj,gjk->abzgk", centered, sym, precision=HI) - dsum
    )
    dfield = lax.optimization_barrier(
        dfield.astype(jnp.bfloat16).reshape(ext_x, ext_y, depth, chans)
    )
    dfield_pad = zwrap(padded_2(dfield, (("gx", 0), ("gy", 1)), 1))
    back = stencil(dfield_pad, kernel, True)
    volume_grad = (upstream.astype(jnp.float32) + back).astype(jnp.bfloat16)
    dfield_own = inner(dfield, edge).astype(jnp.float32)
    ker_terms = []
    for tap in range(27):
        ox, oy, oz = (tap // 9, tap // 3 % 3, tap % 3)
        piece = padded_z[
            edge + ox : edge + ox + size_x, edge + oy : edge + oy + size_y, oz : oz + depth
        ]
        ker_terms.append(jnp.sum(piece.astype(jnp.float32) * dfield_own, axis=(0, 1, 2)))
    ker_part = jnp.stack(ker_terms)
    ker_grad, mix_grad = butterfly_sum((ker_part / scale, mix_part / scale))
    return (output, volume_grad, ker_grad, mix_grad)


def solution(mesh):
    in_specs = (
        P("gx", "gy", None, None),
        P("gx", "gy", None),
        P(),
        P(),
        P(),
        P("gx", "gy", None, None),
    )
    out_specs = (P("gx", "gy", None, None), P("gx", "gy", None, None), P(), P())
    return jax.shard_map(
        per_device, mesh=mesh, in_specs=in_specs, out_specs=out_specs, check_vma=False
    )
```

```python
import jax
import jax.numpy as jnp
from jax import lax
from jax.experimental import pallas as pl
from jax.sharding import PartitionSpec as P

SWEEPS = 5


HI = lax.Precision.HIGHEST
EPS = 1e-05


def padded_2(block, sides, width):
    for axis, dim in sides:
        count = lax.axis_size(axis)
        forward = [(i, i + 1) for i in range(count - 1)]
        forward.append((count - 1, 0))
        backward = [(target, source) for source, target in forward]
        low = lax.ppermute(
            lax.slice_in_dim(block, block.shape[dim] - width, None, axis=dim), axis, forward
        )
        high = lax.ppermute(lax.slice_in_dim(block, 0, width, axis=dim), axis, backward)
        block = jnp.concatenate([low, block, high], axis=dim)
    return block


BUTTERFLY = (("gx", 1), ("gx", 2), ("gx", 4), ("gx", 8), ("gx", 16), ("gx", 32), ("gy", 1), ("gy", 2))


def butterfly(value, combine):
    for axis, bit in BUTTERFLY:
        count = lax.axis_size(axis)
        if bit >= count:
            continue
        pairs = [(i, i ^ bit) for i in range(count)]
        value = combine(value, lax.ppermute(value, axis, pairs))
    return value


def butterfly_sum(parts):
    rows = [p.reshape(-1, 128) for p in parts]
    flat = butterfly(jnp.concatenate(rows, axis=0), lambda a, b: a + b)
    out, start = [], 0
    for p, r in zip(parts, rows):
        out.append(flat[start : start + r.shape[0]].reshape(p.shape))
        start += r.shape[0]
    return out


def pack_moments(n, mean, scat):
    groups, width = mean.shape
    count = jnp.broadcast_to(n.reshape(1, 1, 1), (groups, 1, width))
    return jnp.concatenate([scat, mean[:, None, :], count], axis=1)


def unpack_moments(packed):
    width = packed.shape[2]
    return (packed[:, width + 1 : width + 2], packed[:, width : width + 1], packed[:, :width])


def merge_moments(a, b):
    width = a.shape[2]
    n_a, mean_a, _ = unpack_moments(a)
    n_b, mean_b, _ = unpack_moments(b)
    n = n_a + n_b
    mean = (n_a * mean_a + n_b * mean_b) / n
    delta = mean_b - mean_a
    column = jnp.pad(jnp.swapaxes(delta, 1, 2), ((0, 0), (0, a.shape[1] - width), (0, 0)))
    scat = (a + b) + (n_a * n_b / n) * (column * delta)
    rows = lax.broadcasted_iota(jnp.int32, a.shape, 1)
    fill = jnp.where(rows == width, mean, jnp.where(rows == width + 1, n, 0.0))
    return jnp.where(rows < width, scat, fill)


def whiten(sigma):
    eye = jnp.eye(sigma.shape[0], dtype=sigma.dtype)
    trace = jnp.trace(sigma)
    scaled = sigma / trace
    proj = eye
    for sweep in range(SWEEPS):
        cube = jnp.dot(
            proj, jnp.dot(proj, jnp.dot(proj, scaled, precision=HI), precision=HI), precision=HI
        )
        proj = 1.5 * proj - 0.5 * cube
    return proj / jnp.sqrt(trace)


def mm(a, b):
    return jnp.dot(a, b, precision=HI, preferred_element_type=jnp.float32)


def unit(width):
    rows = lax.broadcasted_iota(jnp.int32, (width, width), 0)
    cols = lax.broadcasted_iota(jnp.int32, (width, width), 1)
    return (rows == cols).astype(jnp.float32)


def whiten_fwd_kernel(sig_ref, white_ref, scaled_ref, ps_ref, as_ref, bs_ref):
    groups, width, _ = sig_ref.shape
    eye = unit(width)
    traces, scaled, proj = [], [], []
    for g in range(groups):
        sig = sig_ref[g]
        trace = jnp.sum(sig * eye, keepdims=True)
        traces.append(trace)
        scaled.append(sig / trace)
        scaled_ref[g] = scaled[g]
        proj.append(eye)
    for sweep in range(SWEEPS):
        first = [mm(proj[g], scaled[g]) for g in range(groups)]
        second = [mm(proj[g], first[g]) for g in range(groups)]
        cube = [mm(proj[g], second[g]) for g in range(groups)]
        for g in range(groups):
            ps_ref[g, sweep] = proj[g]
            as_ref[g, sweep] = first[g]
            bs_ref[g, sweep] = second[g]
            proj[g] = 1.5 * proj[g] - 0.5 * cube[g]
    for g in range(groups):
        ps_ref[g, SWEEPS] = proj[g]
        white_ref[g] = proj[g] / jnp.sqrt(traces[g])


def whiten_bwd_kernel(sig_ref, scaled_ref, ps_ref, as_ref, bs_ref, dwhite_ref, sens_ref):
    groups, width, _ = sig_ref.shape
    eye = unit(width)
    traces, roots, grad, grad_trace, grad_scaled = [], [], [], [], []
    for g in range(groups):
        sig = sig_ref[g]
        trace = jnp.sum(sig * eye, keepdims=True)
        root = jnp.sqrt(trace)
        dwhite = dwhite_ref[g]
        traces.append(trace)
        grad.append(dwhite / root)
        grad_trace.append(-0.5 * jnp.sum(dwhite * ps_ref[g, SWEEPS], keepdims=True) / (trace * root))
        grad_scaled.append(jnp.zeros_like(sig))
    for sweep in reversed(range(SWEEPS)):
        proj = [ps_ref[g, sweep] for g in range(groups)]
        grad_cube = [-0.5 * grad[g] for g in range(groups)]
        grad_second = [mm(proj[g], grad_cube[g]) for g in range(groups)]
        grad_first = [mm(proj[g], grad_second[g]) for g in range(groups)]
        for g in range(groups):
            grad_scaled[g] = grad_scaled[g] + mm(proj[g], grad_first[g])
            grad[g] = (
                1.5 * grad[g]
                + mm(grad_cube[g], bs_ref[g, sweep])
                + mm(grad_second[g], as_ref[g, sweep])
                + mm(grad_first[g], scaled_ref[g])
            )
    for g in range(groups):
        trace = traces[g]
        total = grad_trace[g] - jnp.sum(grad_scaled[g] * sig_ref[g], keepdims=True) / (trace * trace)
        sens_ref[g] = grad_scaled[g] / trace + total * eye


def whiten_fwd(sigma):
    groups, width, _ = sigma.shape
    f32 = jnp.float32
    return pl.pallas_call(
        whiten_fwd_kernel,
        out_shape=[
            jax.ShapeDtypeStruct((groups, width, width), f32),
            jax.ShapeDtypeStruct((groups, width, width), f32),
            jax.ShapeDtypeStruct((groups, SWEEPS + 1, width, width), f32),
            jax.ShapeDtypeStruct((groups, SWEEPS, width, width), f32),
            jax.ShapeDtypeStruct((groups, SWEEPS, width, width), f32),
        ],
    )(sigma)


def whiten_bwd(sigma, scaled, ps, as_, bs, dwhite):
    groups, width, _ = sigma.shape
    return pl.pallas_call(
        whiten_bwd_kernel,
        out_shape=jax.ShapeDtypeStruct((groups, width, width), jnp.float32),
    )(sigma, scaled, ps, as_, bs, dwhite)


def zwrap(field):
    return jnp.concatenate([field[:, :, -1:], field, field[:, :, :1]], axis=2)


def stencil(padded, kernel, flip):
    size_x, size_y, depth = (padded.shape[0] - 2, padded.shape[1] - 2, padded.shape[2] - 2)
    taps = kernel.astype(jnp.float32)
    total = jnp.zeros((size_x, size_y, depth, padded.shape[3]), jnp.float32)
    for tap in range(27):
        ox, oy, oz = (tap // 9, tap // 3 % 3, tap % 3)
        if flip:
            ox, oy, oz = (2 - ox, 2 - oy, 2 - oz)
        piece = padded[ox : ox + size_x, oy : oy + size_y, oz : oz + depth]
        total = total + piece.astype(jnp.float32) * taps[tap]
    return total


def inner(field, edge):
    return field[edge : field.shape[0] - edge, edge : field.shape[1] - edge]


def per_device(volume, void_mask, kernel, mix_weight, norm_gain, upstream):
    size_x, size_y, depth, chans = volume.shape
    groups, width = (mix_weight.shape[0], mix_weight.shape[1])
    scale = jnp.float32(size_x * size_y * depth * lax.axis_size("gx") * lax.axis_size("gy"))
    keep_own = (1 - void_mask).astype(jnp.float32)
    rim = 1
    padded_x = padded_2(volume, (("gx", 0), ("gy", 1)), 1)
    edge = rim - 1
    padded_z = zwrap(padded_x)
    field = lax.optimization_barrier(stencil(padded_z, kernel, False).astype(jnp.bfloat16)).astype(
        jnp.float32
    )
    ext_x, ext_y = (field.shape[0], field.shape[1])
    field_own = inner(field, edge)
    masked_own = keep_own[..., None] * field_own
    count_part = jnp.sum(keep_own)
    sum_part = jnp.sum(masked_own, axis=(0, 1, 2))
    eye = jnp.eye(width, dtype=jnp.float32)
    mean_part = (sum_part / count_part).reshape(groups, width)
    cent_part = field_own.reshape(size_x, size_y, depth, groups, width) - mean_part
    cov_part = jnp.einsum(
        "abzgi,abzgj->gij", keep_own[..., None, None] * cent_part, cent_part, precision=HI
    )
    moments = butterfly(pack_moments(count_part, mean_part, cov_part), merge_moments)
    count, mean, scatter = unpack_moments(moments)
    count = count[0, 0, 0]
    mean = mean[:, 0]
    sigma = scatter / count + EPS * eye
    white, scaled, ps, as_, bs = whiten_fwd(sigma)
    centered = field.reshape(ext_x, ext_y, depth, groups, width) - mean
    gain = norm_gain.reshape(groups, width)
    pre = jnp.einsum("abzgj,gij->abzgi", centered, white, precision=HI) * gain
    active = jax.nn.silu(pre).astype(jnp.bfloat16)
    active_own = inner(active, edge)
    grad_five = upstream.reshape(ext_x, ext_y, depth, groups, width)
    mixed = jnp.einsum(
        "abzgi,gio->abzgo", active_own, mix_weight, preferred_element_type=jnp.float32
    )
    output = (volume.astype(jnp.float32) + mixed.reshape(size_x, size_y, depth, chans)).astype(
        jnp.bfloat16
    )
    mix_part = jnp.einsum(
        "abzgi,abzgo->gio",
        active_own,
        upstream.reshape(size_x, size_y, depth, groups, width),
        preferred_element_type=jnp.float32,
    )
    dact = jnp.einsum("abzgo,gio->abzgi", grad_five, mix_weight, preferred_element_type=jnp.float32)
    sig = jax.nn.sigmoid(pre)
    dnormed = dact * sig * (1.0 + pre * (1.0 - sig)) * gain
    dcent = jnp.einsum("abzgi,gij->abzgj", dnormed, white, precision=HI)
    dwhite_part = jnp.einsum(
        "abzgi,abzgj->gij", inner(dnormed, edge), inner(centered, edge), precision=HI
    )
    dsum_part = jnp.einsum(
        "gi,gij->gj", jnp.sum(inner(dnormed, edge), axis=(0, 1, 2)), white, precision=HI
    )
    dwhite, dsum = butterfly_sum((dwhite_part, dsum_part))
    sens = whiten_bwd(sigma, scaled, ps, as_, bs, dwhite)
    sym = sens + jnp.swapaxes(sens, 1, 2)
    dfield = dcent + keep_own[..., None, None] / count * (
        jnp.einsum("abzgj,gjk->abzgk", centered, sym, precision=HI) - dsum
    )
    dfield = lax.optimization_barrier(
        dfield.astype(jnp.bfloat16).reshape(ext_x, ext_y, depth, chans)
    )
    dfield_pad = zwrap(padded_2(dfield, (("gx", 0), ("gy", 1)), 1))
    back = stencil(dfield_pad, kernel, True)
    volume_grad = (upstream.astype(jnp.float32) + back).astype(jnp.bfloat16)
    dfield_own = inner(dfield, edge).astype(jnp.float32)
    ker_terms = []
    for tap in range(27):
        ox, oy, oz = (tap // 9, tap // 3 % 3, tap % 3)
        piece = padded_z[
            edge + ox : edge + ox + size_x, edge + oy : edge + oy + size_y, oz : oz + depth
        ]
        ker_terms.append(jnp.sum(piece.astype(jnp.float32) * dfield_own, axis=(0, 1, 2)))
    ker_part = jnp.stack(ker_terms)
    ker_sum, mix_sum = butterfly_sum((ker_part, mix_part))
    return (output, volume_grad, ker_sum / scale, mix_sum / scale)


def solution(mesh):
    in_specs = (
        P("gx", "gy", None, None),
        P("gx", "gy", None),
        P(),
        P(),
        P(),
        P("gx", "gy", None, None),
    )
    out_specs = (P("gx", "gy", None, None), P("gx", "gy", None, None), P(), P())
    return jax.shard_map(
        per_device, mesh=mesh, in_specs=in_specs, out_specs=out_specs, check_vma=False
    )
```

```python
import jax
import jax.numpy as jnp
from jax import lax
from jax.experimental import pallas as pl
from jax.sharding import PartitionSpec as P

SWEEPS = 5


HI = lax.Precision.HIGHEST
EPS = 1e-05


def padded_2(block, sides, width):
    for axis, dim in sides:
        count = lax.axis_size(axis)
        forward = [(i, i + 1) for i in range(count - 1)]
        forward.append((count - 1, 0))
        backward = [(target, source) for source, target in forward]
        low = lax.ppermute(
            lax.slice_in_dim(block, block.shape[dim] - width, None, axis=dim), axis, forward
        )
        high = lax.ppermute(lax.slice_in_dim(block, 0, width, axis=dim), axis, backward)
        block = jnp.concatenate([low, block, high], axis=dim)
    return block


BUTTERFLY = (("gx", 1), ("gx", 2), ("gx", 4), ("gx", 8), ("gx", 16), ("gx", 32), ("gy", 1), ("gy", 2))


def butterfly(value, combine):
    for axis, bit in BUTTERFLY:
        count = lax.axis_size(axis)
        if bit >= count:
            continue
        pairs = [(i, i ^ bit) for i in range(count)]
        value = combine(value, lax.ppermute(value, axis, pairs))
    return value


def butterfly_sum(parts):
    rows = [p.reshape(-1, 128) for p in parts]
    flat = butterfly(jnp.concatenate(rows, axis=0), lambda a, b: a + b)
    out, start = [], 0
    for p, r in zip(parts, rows):
        out.append(flat[start : start + r.shape[0]].reshape(p.shape))
        start += r.shape[0]
    return out


def pack_moments(n, mean, scat):
    groups, width = mean.shape
    count = jnp.broadcast_to(n.reshape(1, 1, 1), (groups, 1, width))
    return jnp.concatenate([scat, mean[:, None, :], count], axis=1)


def unpack_moments(packed):
    width = packed.shape[2]
    return (packed[:, width + 1 : width + 2], packed[:, width : width + 1], packed[:, :width])


def merge_moments(a, b):
    width = a.shape[2]
    n_a, mean_a, _ = unpack_moments(a)
    n_b, mean_b, _ = unpack_moments(b)
    n = n_a + n_b
    mean = (n_a * mean_a + n_b * mean_b) / n
    delta = mean_b - mean_a
    column = jnp.pad(jnp.swapaxes(delta, 1, 2), ((0, 0), (0, a.shape[1] - width), (0, 0)))
    scat = (a + b) + (n_a * n_b / n) * (column * delta)
    rows = lax.broadcasted_iota(jnp.int32, a.shape, 1)
    fill = jnp.where(rows == width, mean, jnp.where(rows == width + 1, n, 0.0))
    return jnp.where(rows < width, scat, fill)


def whiten(sigma):
    eye = jnp.eye(sigma.shape[0], dtype=sigma.dtype)
    trace = jnp.trace(sigma)
    scaled = sigma / trace
    proj = eye
    for sweep in range(SWEEPS):
        cube = jnp.dot(
            proj, jnp.dot(proj, jnp.dot(proj, scaled, precision=HI), precision=HI), precision=HI
        )
        proj = 1.5 * proj - 0.5 * cube
    return proj / jnp.sqrt(trace)


def mm(a, b):
    return jnp.dot(a, b, precision=HI, preferred_element_type=jnp.float32)


def unit(width):
    rows = lax.broadcasted_iota(jnp.int32, (width, width), 0)
    cols = lax.broadcasted_iota(jnp.int32, (width, width), 1)
    return (rows == cols).astype(jnp.float32)


def whiten_fwd_kernel(sig_ref, white_ref, scaled_ref, ps_ref, as_ref, bs_ref):
    groups, width, _ = sig_ref.shape
    eye = unit(width)
    traces, scaled, proj = [], [], []
    for g in range(groups):
        sig = sig_ref[g]
        trace = jnp.sum(sig * eye, keepdims=True)
        traces.append(trace)
        scaled.append(sig / trace)
        scaled_ref[g] = scaled[g]
        proj.append(eye)
    for sweep in range(SWEEPS):
        first = [mm(proj[g], scaled[g]) for g in range(groups)]
        second = [mm(proj[g], first[g]) for g in range(groups)]
        cube = [mm(proj[g], second[g]) for g in range(groups)]
        for g in range(groups):
            ps_ref[g, sweep] = proj[g]
            as_ref[g, sweep] = first[g]
            bs_ref[g, sweep] = second[g]
            proj[g] = 1.5 * proj[g] - 0.5 * cube[g]
    for g in range(groups):
        ps_ref[g, SWEEPS] = proj[g]
        white_ref[g] = proj[g] / jnp.sqrt(traces[g])


def whiten_bwd_kernel(sig_ref, scaled_ref, ps_ref, as_ref, bs_ref, dwhite_ref, sens_ref):
    groups, width, _ = sig_ref.shape
    eye = unit(width)
    traces, roots, grad, grad_trace, grad_scaled = [], [], [], [], []
    for g in range(groups):
        sig = sig_ref[g]
        trace = jnp.sum(sig * eye, keepdims=True)
        root = jnp.sqrt(trace)
        dwhite = dwhite_ref[g]
        traces.append(trace)
        grad.append(dwhite / root)
        grad_trace.append(-0.5 * jnp.sum(dwhite * ps_ref[g, SWEEPS], keepdims=True) / (trace * root))
        grad_scaled.append(jnp.zeros_like(sig))
    for sweep in reversed(range(SWEEPS)):
        proj = [ps_ref[g, sweep] for g in range(groups)]
        grad_cube = [-0.5 * grad[g] for g in range(groups)]
        grad_second = [mm(proj[g], grad_cube[g]) for g in range(groups)]
        grad_first = [mm(proj[g], grad_second[g]) for g in range(groups)]
        for g in range(groups):
            grad_scaled[g] = grad_scaled[g] + mm(proj[g], grad_first[g])
            grad[g] = (
                1.5 * grad[g]
                + mm(grad_cube[g], bs_ref[g, sweep])
                + mm(grad_second[g], as_ref[g, sweep])
                + mm(grad_first[g], scaled_ref[g])
            )
    for g in range(groups):
        trace = traces[g]
        total = grad_trace[g] - jnp.sum(grad_scaled[g] * sig_ref[g], keepdims=True) / (trace * trace)
        sens_ref[g] = grad_scaled[g] / trace + total * eye


def whiten_fwd(sigma):
    groups, width, _ = sigma.shape
    f32 = jnp.float32
    return pl.pallas_call(
        whiten_fwd_kernel,
        out_shape=[
            jax.ShapeDtypeStruct((groups, width, width), f32),
            jax.ShapeDtypeStruct((groups, width, width), f32),
            jax.ShapeDtypeStruct((groups, SWEEPS + 1, width, width), f32),
            jax.ShapeDtypeStruct((groups, SWEEPS, width, width), f32),
            jax.ShapeDtypeStruct((groups, SWEEPS, width, width), f32),
        ],
    )(sigma)


def whiten_bwd(sigma, scaled, ps, as_, bs, dwhite):
    groups, width, _ = sigma.shape
    return pl.pallas_call(
        whiten_bwd_kernel,
        out_shape=jax.ShapeDtypeStruct((groups, width, width), jnp.float32),
    )(sigma, scaled, ps, as_, bs, dwhite)


def zwrap(field):
    return jnp.concatenate([field[:, :, -1:], field, field[:, :, :1]], axis=2)


def stencil(padded, kernel, flip):
    size_x, size_y, depth = (padded.shape[0] - 2, padded.shape[1] - 2, padded.shape[2] - 2)
    taps = kernel.astype(jnp.float32)
    total = jnp.zeros((size_x, size_y, depth, padded.shape[3]), jnp.float32)
    for tap in range(27):
        ox, oy, oz = (tap // 9, tap // 3 % 3, tap % 3)
        if flip:
            ox, oy, oz = (2 - ox, 2 - oy, 2 - oz)
        piece = padded[ox : ox + size_x, oy : oy + size_y, oz : oz + depth]
        total = total + piece.astype(jnp.float32) * taps[tap]
    return total


def inner(field, edge):
    return field[edge : field.shape[0] - edge, edge : field.shape[1] - edge]


def per_device(volume, void_mask, kernel, mix_weight, norm_gain, upstream):
    size_x, size_y, depth, chans = volume.shape
    groups, width = (mix_weight.shape[0], mix_weight.shape[1])
    scale = jnp.float32(size_x * size_y * depth * lax.axis_size("gx") * lax.axis_size("gy"))
    keep_own = (1 - void_mask).astype(jnp.float32)
    rim = 1
    padded_x = padded_2(volume, (("gx", 0), ("gy", 1)), 1)
    edge = rim - 1
    padded_z = zwrap(padded_x)
    field = lax.optimization_barrier(stencil(padded_z, kernel, False).astype(jnp.bfloat16)).astype(
        jnp.float32
    )
    ext_x, ext_y = (field.shape[0], field.shape[1])
    field_own = inner(field, edge)
    masked_own = keep_own[..., None] * field_own
    count_part = jnp.sum(keep_own)
    sum_part = jnp.sum(masked_own, axis=(0, 1, 2))
    eye = jnp.eye(width, dtype=jnp.float32)
    mean_part = (sum_part / count_part).reshape(groups, width)
    cent_part = field_own.reshape(size_x, size_y, depth, groups, width) - mean_part
    cov_part = jnp.einsum(
        "abzgi,abzgj->gij", keep_own[..., None, None] * cent_part, cent_part, precision=HI
    )
    moments = butterfly(pack_moments(count_part, mean_part, cov_part), merge_moments)
    count, mean, scatter = unpack_moments(moments)
    count = count[0, 0, 0]
    mean = mean[:, 0]
    sigma = scatter / count + EPS * eye
    white, scaled, ps, as_, bs = whiten_fwd(sigma)
    centered = field.reshape(ext_x, ext_y, depth, groups, width) - mean
    gain = norm_gain.reshape(groups, width)
    pre = jnp.einsum("abzgj,gij->abzgi", centered, white, precision=HI) * gain
    active = jax.nn.silu(pre).astype(jnp.bfloat16)
    active_own = inner(active, edge)
    grad_five = upstream.reshape(ext_x, ext_y, depth, groups, width)
    mixed = jnp.einsum(
        "abzgi,gio->abzgo", active_own, mix_weight, preferred_element_type=jnp.float32
    )
    output = (volume.astype(jnp.float32) + mixed.reshape(size_x, size_y, depth, chans)).astype(
        jnp.bfloat16
    )
    mix_part = jnp.einsum(
        "abzgi,abzgo->gio",
        active_own,
        upstream.reshape(size_x, size_y, depth, groups, width),
        preferred_element_type=jnp.float32,
    )
    dact = jnp.einsum("abzgo,gio->abzgi", grad_five, mix_weight, preferred_element_type=jnp.float32)
    sig = jax.nn.sigmoid(pre)
    dnormed = dact * sig * (1.0 + pre * (1.0 - sig)) * gain
    dcent = jnp.einsum("abzgi,gij->abzgj", dnormed, white, precision=HI)
    dwhite_part = jnp.einsum(
        "abzgi,abzgj->gij", inner(dnormed, edge), inner(centered, edge), precision=HI
    )
    dsum_part = jnp.einsum(
        "gi,gij->gj", jnp.sum(inner(dnormed, edge), axis=(0, 1, 2)), white, precision=HI
    )
    dwhite, dsum = butterfly_sum((dwhite_part, dsum_part))
    sens = whiten_bwd(sigma, scaled, ps, as_, bs, dwhite)
    sym = sens + jnp.swapaxes(sens, 1, 2)
    dfield = dcent + keep_own[..., None, None] / count * (
        jnp.einsum("abzgj,gjk->abzgk", centered, sym, precision=HI) - dsum
    )
    dfield = lax.optimization_barrier(
        dfield.astype(jnp.bfloat16).reshape(ext_x, ext_y, depth, chans)
    )
    dfield_pad = zwrap(padded_2(dfield, (("gx", 0), ("gy", 1)), 1))
    back = stencil(dfield_pad, kernel, True)
    volume_grad = (upstream.astype(jnp.float32) + back).astype(jnp.bfloat16)
    dfield_own = inner(dfield, edge).astype(jnp.float32)
    ker_terms = []
    for tap in range(27):
        ox, oy, oz = (tap // 9, tap // 3 % 3, tap % 3)
        piece = padded_z[
            edge + ox : edge + ox + size_x, edge + oy : edge + oy + size_y, oz : oz + depth
        ]
        ker_terms.append(jnp.sum(piece.astype(jnp.float32) * dfield_own, axis=(0, 1, 2)))
    ker_part = jnp.stack(ker_terms)
    ker_grad, mix_grad = butterfly_sum((ker_part / scale, mix_part / scale))
    return (output, volume_grad, ker_grad, mix_grad)


def solution(mesh):
    in_specs = (
        P("gx", "gy", None, None),
        P("gx", "gy", None),
        P(),
        P(),
        P(),
        P("gx", "gy", None, None),
    )
    out_specs = (P("gx", "gy", None, None), P("gx", "gy", None, None), P(), P())
    return jax.shard_map(
        per_device, mesh=mesh, in_specs=in_specs, out_specs=out_specs, check_vma=False
    )
```
